32 devices in a mesh: dp: 4 (over z), fsdp: 2 (over x), rows: 4 (over y, core).
Axes of the slice: x: 2, y: 2, z: 4, core: 2. Of those that a mesh axis runs over, the one named last changes fastest.
Arguments:
- feature_maps: bfloat16 [8, 16, 32, 1536], P(('dp', 'fsdp'), 'rows'), may hold values from -30 to 30
- dw_kernel: float32 [7, 7, 1536], replicated, may hold values from -0.875 to 0.875
- norm_gain: float32 [1536], replicated, may hold values from 0.5 to 1.5
- w_up: bfloat16 [1536, 6144], P(('dp', 'rows'), 'fsdp'), may hold values from -0.15625 to 0.15625
- w_down: bfloat16 [6144, 1536], P('fsdp', ('dp', 'rows')), may hold values from -0.078125 to 0.078125
- layer_scale: float32 [1536], replicated, may hold values from 0.3 to 1.5
- d_out: bfloat16 [8, 16, 32, 1536], P(('dp', 'fsdp'), 'rows'), may hold values from -20 to 20
Outputs:
- result: bfloat16 [8, 16, 32, 1536], P(('dp', 'fsdp'), 'rows')
- grad_x: bfloat16 [8, 16, 32, 1536], P(('dp', 'fsdp'), 'rows')
- grad_up: float32 [1536, 6144], P(('dp', 'rows'), 'fsdp')
- grad_down: float32 [6144, 1536], P('fsdp', ('dp', 'rows'))
- grad_kernel: float32 [7, 7, 1536], replicated
- grad_gain: float32 [1536], replicated
- grad_scale: float32 [1536], replicated
The draws below stay inside these ranges and needn't reach their ends.
All inputs are finite; a program needn't handle non-finite values.
Results may differ from the reference program's by a relative error of at most 0.0075.
Values may be sent and summed in bfloat16 or wider, within the bound.
No kernel may reach another device: no remote copies, remote signals or barrier semaphores. Data moves between devices by JAX's collectives and lax.ppermute only.
A program may use at most 128 MiB of HBM per device.

```python
import math
import jax
import jax.numpy as jnp
from jax import lax

C = 1536
HID = 6144
KS = 7
MAP_W = 32
SCENES = 8
MAP_H = 16


def draw_feature_maps(key, part):
    first, second, third = jax.random.split(jax.random.fold_in(key, 11), 3)
    shape = (SCENES, MAP_H, MAP_W, C)
    channel_scale = jnp.exp(jax.random.uniform(first, (C,), jnp.float32, math.log(0.5), math.log(5.0)))
    cell_scale = jnp.exp(jax.random.uniform(second, (SCENES, MAP_H, MAP_W, 1), jnp.float32, math.log(0.5), math.log(2.0)))
    base = jnp.clip(jax.random.normal(third, shape, jnp.float32), -6.0, 6.0)
    return jnp.clip(base * channel_scale * cell_scale, -30.0, 30.0).astype(jnp.bfloat16)


def draw_d_out(key, part):
    first = jax.random.fold_in(jax.random.fold_in(key, 23), 0)
    shape = (SCENES, MAP_H, MAP_W, C)
    scene_pos = jnp.arange(SCENES, dtype=jnp.float32).reshape(SCENES, 1, 1, 1)
    row_pos = jnp.arange(MAP_H, dtype=jnp.float32).reshape(1, MAP_H, 1, 1)
    rising = jnp.exp(math.log(3.0) * (scene_pos * MAP_H + row_pos) / (SCENES * MAP_H))
    base = jnp.clip(jax.random.normal(first, shape, jnp.float32), -6.0, 6.0)
    return jnp.clip(base * rising, -20.0, 20.0).astype(jnp.bfloat16)


def shard_levels(own_key, shape, cuts, least, high):
    level, own = 1.0, jax.random.fold_in(own_key, 6)
    for position, shards_of in cuts:
        steps = jnp.exp(jax.random.uniform(jax.random.fold_in(own, position), (shards_of,), jnp.float32, least / len(cuts), high / len(cuts)))
        level = level * jnp.repeat(steps, shape[position] // shards_of).reshape([-1 if axis == position else 1 for axis in range(len(shape))])
    return level


def scatter_about(own_key, shape, scale, most, pieces=(), kind=jnp.bfloat16):
    drawn = jax.random.normal(own_key, shape, jnp.float32) * scale
    if len(pieces) > 0:
        drawn = shard_levels(own_key, shape, pieces, -0.22, 0.18) * drawn
    return jnp.clip(drawn, min=-most, max=most).astype(kind)


def setup_inputs(seed: int = 0) -> dict:
    splits = jax.random.split(jax.random.key(seed), 8)
    return {
        "feature_maps": draw_feature_maps(jax.random.fold_in(splits[7], 71), 0),
        "dw_kernel": scatter_about(splits[1], (KS, KS, C), (KS * KS) ** -0.5, 0.875, (), jnp.float32),
        "norm_gain": jnp.clip(1.0 + 0.1 * jax.random.normal(splits[2], (C,), jnp.float32), 0.5, 1.5),
        "w_up": scatter_about(splits[3], (C, HID), C ** -0.5, 0.15625, ((0, 16), (1, 2))),
        "w_down": scatter_about(splits[4], (HID, C), HID ** -0.5, 0.078125, ((0, 2), (1, 16))),
        "layer_scale": jnp.clip(jnp.exp(jax.random.uniform(splits[5], (C,), jnp.float32, math.log(0.3), math.log(1.5))), 0.3, 1.5),
        "d_out": draw_d_out(jax.random.fold_in(splits[7], 71), 0),
    }


norm_eps = 1e-06
inv_root_two = 1.0 / math.sqrt(2.0)
inv_root_two_pi = 1.0 / math.sqrt(2.0 * math.pi)

def gelu_exact(values):
    return 0.5 * values * (1.0 + jax.scipy.special.erf(values * inv_root_two))

def gelu_slope(values):
    cdf_part = 0.5 * (1.0 + jax.scipy.special.erf(values * inv_root_two))
    return cdf_part + values * jnp.exp(-0.5 * values * values) * inv_root_two_pi

def reference(feature_maps, dw_kernel, norm_gain, w_up, w_down, layer_scale, d_out):
    scenes, height, across, width = feature_maps.shape
    resid = feature_maps.astype(jnp.float32)
    padded = jnp.pad(resid, ((0, 0), (3, 3), (3, 3), (0, 0)))
    filtered = jnp.zeros(feature_maps.shape, jnp.float32)
    for row_off in range(KS):
        for col_off in range(KS):
            filtered = filtered + padded[:, row_off:row_off + height, col_off:col_off + across, :] * dw_kernel[row_off, col_off]
    flat = filtered.reshape(-1, width)
    average = lax.optimization_barrier(jnp.mean(flat, axis=-1, keepdims=True))
    center = flat - average
    variance = lax.optimization_barrier(jnp.mean(center * center, axis=-1, keepdims=True))
    rstd = lax.rsqrt(variance + norm_eps)
    normed = center * rstd
    scaled = (normed * norm_gain).astype(jnp.bfloat16)
    hidden = jnp.dot(scaled, w_up, preferred_element_type=jnp.float32)
    active = gelu_exact(hidden).astype(jnp.bfloat16)
    branch = jnp.dot(active, w_down, preferred_element_type=jnp.float32)
    result = (resid.reshape(-1, width) + layer_scale * branch).astype(jnp.bfloat16).reshape(feature_maps.shape)
    cotan = d_out.astype(jnp.float32).reshape(-1, width)
    back = (cotan * layer_scale).astype(jnp.bfloat16)
    grad_scale = lax.optimization_barrier(jnp.sum(cotan * branch, axis=0))
    grad_down = jnp.dot(active.T, back, preferred_element_type=jnp.float32)
    slope_in = jnp.dot(back, w_down.T, preferred_element_type=jnp.float32)
    hidden_grad = (slope_in * gelu_slope(hidden)).astype(jnp.bfloat16)
    grad_up = jnp.dot(scaled.T, hidden_grad, preferred_element_type=jnp.float32)
    norm_grad = jnp.dot(hidden_grad, w_up.T, preferred_element_type=jnp.float32)
    grad_gain = lax.optimization_barrier(jnp.sum(norm_grad * normed, axis=0))
    scaled_grad = norm_grad * norm_gain
    conv_grad = rstd * (scaled_grad - lax.optimization_barrier(jnp.mean(scaled_grad, axis=-1, keepdims=True)) - normed * lax.optimization_barrier(jnp.mean(scaled_grad * normed, axis=-1, keepdims=True)))
    conv_grad = conv_grad.reshape(feature_maps.shape)
    grad_pad = jnp.pad(conv_grad, ((0, 0), (3, 3), (3, 3), (0, 0)))
    kernel_rows = []
    back_conv = jnp.zeros(feature_maps.shape, jnp.float32)
    for row_off in range(KS):
        for col_off in range(KS):
            window = padded[:, row_off:row_off + height, col_off:col_off + across, :]
            kernel_rows.append(lax.optimization_barrier(jnp.sum(window * conv_grad, axis=(0, 1, 2))))
            back_conv = back_conv + grad_pad[:, 6 - row_off:6 - row_off + height, 6 - col_off:6 - col_off + across, :] * dw_kernel[row_off, col_off]
    grad_kernel = jnp.stack(kernel_rows).reshape(KS, KS, width)
    grad_x = (d_out.astype(jnp.float32) + back_conv).astype(jnp.bfloat16)
    return (result, grad_x, grad_up, grad_down, grad_kernel, grad_gain, grad_scale)
```

```python
import math

import jax
import jax.numpy as jnp
from jax import lax
from jax.sharding import PartitionSpec as P

KS = 7


norm_eps = 1e-06
inv_root_two = 1.0 / math.sqrt(2.0)
inv_root_two_pi = 1.0 / math.sqrt(2.0 * math.pi)
contract_rows = (((0,), (0,)), ((), ()))
contract_cols = (((1,), (1,)), ((), ()))


def padded_2(x, sides, width):
    for axis, dim in sides:
        devices, length = (lax.axis_size(axis), x.shape[dim])
        up = [(i, (i + 1) % devices) for i in range(devices - 1)]
        down = [(j, i) for i, j in up]
        last = lax.slice_in_dim(x, length - width, length, axis=dim)
        leading = lax.slice_in_dim(x, 0, width, axis=dim)
        before = lax.ppermute(last, axis, up)
        after = lax.ppermute(leading, axis, down)
        x = jnp.concatenate([before, x, after], axis=dim)
    return x


def gelu_exact(values):
    return 0.5 * values * (1.0 + jax.scipy.special.erf(values * inv_root_two))


def gelu_slope(values):
    cdf_part = 0.5 * (1.0 + jax.scipy.special.erf(values * inv_root_two))
    return cdf_part + values * jnp.exp(-0.5 * values * values) * inv_root_two_pi


def body(feature_maps, dw_kernel, norm_gain, w_up, w_down, layer_scale, d_out):
    scenes, strip, across, width = feature_maps.shape
    cells = scenes * strip * across
    hid_axes = ("fsdp", "rows")
    up_loc = lax.all_to_all(w_up, "rows", 1, 0, tiled=True)
    up_loc = lax.all_gather(up_loc, "dp", axis=0, tiled=True)
    down_loc = lax.all_to_all(w_down, "rows", 0, 1, tiled=True)
    down_loc = lax.all_gather(down_loc, "dp", axis=1, tiled=True)
    cotan = d_out.reshape(cells, width).astype(jnp.float32)
    back = (cotan * layer_scale).astype(jnp.bfloat16)
    back_all = lax.all_gather(back, hid_axes, axis=0, tiled=True)
    rimmed = padded_2(feature_maps, (("rows", 1),), 3)
    padded = jnp.pad(rimmed.astype(jnp.float32), ((0, 0), (0, 0), (3, 3), (0, 0)))
    filtered = jnp.zeros(feature_maps.shape, jnp.float32)
    for row_off in range(KS):
        for col_off in range(KS):
            filtered = (
                filtered
                + padded[:, row_off : row_off + strip, col_off : col_off + across, :]
                * dw_kernel[row_off, col_off]
            )
    flat = filtered.reshape(cells, width)
    average = jnp.mean(flat, axis=-1, keepdims=True)
    center = flat - average
    variance = jnp.mean(center * center, axis=-1, keepdims=True)
    rstd = lax.rsqrt(variance + norm_eps)
    normed = center * rstd
    scaled = (normed * norm_gain).astype(jnp.bfloat16)
    gathered = lax.all_gather(scaled, hid_axes, axis=0, tiled=True)
    hidden = jnp.dot(gathered, up_loc, preferred_element_type=jnp.float32)
    active = gelu_exact(hidden).astype(jnp.bfloat16)
    mlp_terms = jnp.dot(active, down_loc, preferred_element_type=jnp.float32)
    branch = lax.psum_scatter(
        mlp_terms.astype(jnp.bfloat16), hid_axes, scatter_dimension=0, tiled=True
    ).astype(jnp.float32)
    resid = feature_maps.reshape(cells, width).astype(jnp.float32)
    result = (resid + layer_scale * branch).astype(jnp.bfloat16).reshape(feature_maps.shape)
    scale_part = jnp.sum(cotan * branch, axis=0)
    down_part = lax.dot_general(active, back_all, contract_rows, preferred_element_type=jnp.float32)
    slope_in = lax.dot_general(
        back_all, down_loc, contract_cols, preferred_element_type=jnp.float32
    )
    hidden_grad = (slope_in * gelu_slope(hidden)).astype(jnp.bfloat16)
    up_part = lax.dot_general(
        gathered, hidden_grad, contract_rows, preferred_element_type=jnp.float32
    )
    norm_terms = lax.dot_general(
        hidden_grad, up_loc, contract_cols, preferred_element_type=jnp.float32
    )
    norm_grad = lax.psum_scatter(norm_terms, hid_axes, scatter_dimension=0, tiled=True)
    grad_up = lax.psum_scatter(up_part, "dp", scatter_dimension=0, tiled=True)
    grad_up = lax.all_to_all(grad_up, "rows", 0, 1, tiled=True)
    grad_down = lax.psum_scatter(down_part, "dp", scatter_dimension=1, tiled=True)
    grad_down = lax.all_to_all(grad_down, "rows", 1, 0, tiled=True)
    gain_part = jnp.sum(norm_grad * normed, axis=0)
    scaled_grad = norm_grad * norm_gain
    conv_grad = rstd * (
        scaled_grad
        - jnp.mean(scaled_grad, axis=-1, keepdims=True)
        - normed * jnp.mean(scaled_grad * normed, axis=-1, keepdims=True)
    )
    conv_grad = conv_grad.reshape(feature_maps.shape)
    grad_rim = padded_2(conv_grad.astype(jnp.bfloat16), (("rows", 1),), 3).astype(conv_grad.dtype)
    grad_pad = jnp.pad(grad_rim, ((0, 0), (0, 0), (3, 3), (0, 0)))
    kernel_rows = []
    back_conv = jnp.zeros(feature_maps.shape, jnp.float32)
    for row_off in range(KS):
        for col_off in range(KS):
            window = padded[:, row_off : row_off + strip, col_off : col_off + across, :]
            kernel_rows.append(jnp.sum(window * conv_grad, axis=(0, 1, 2)))
            back_conv = (
                back_conv
                + grad_pad[
                    :, 6 - row_off : 6 - row_off + strip, 6 - col_off : 6 - col_off + across, :
                ]
                * dw_kernel[row_off, col_off]
            )
    kernel_part = jnp.stack(kernel_rows).reshape(KS, KS, width)
    grad_x = (d_out.astype(jnp.float32) + back_conv).astype(jnp.bfloat16)
    grad_kernel, grad_gain, grad_scale = lax.psum(
        (kernel_part, gain_part, scale_part), ("dp", "fsdp", "rows")
    )
    return (result, grad_x, grad_up, grad_down, grad_kernel, grad_gain, grad_scale)


def solution(mesh):
    return jax.shard_map(
        body,
        mesh=mesh,
        in_specs=(
            P(("dp", "fsdp"), "rows", None, None),
            P(),
            P(),
            P(("dp", "rows"), "fsdp"),
            P("fsdp", ("dp", "rows")),
            P(),
            P(("dp", "fsdp"), "rows", None, None),
        ),
        out_specs=(
            P(("dp", "fsdp"), "rows", None, None),
            P(("dp", "fsdp"), "rows", None, None),
            P(("dp", "rows"), "fsdp"),
            P("fsdp", ("dp", "rows")),
            P(),
            P(),
            P(),
        ),
        check_vma=False,
    )
```

```python
import math

import jax
import jax.numpy as jnp
from jax import lax
from jax.sharding import PartitionSpec as P

KS = 7


norm_eps = 1e-06
inv_root_two = 1.0 / math.sqrt(2.0)
inv_root_two_pi = 1.0 / math.sqrt(2.0 * math.pi)
contract_rows = (((0,), (0,)), ((), ()))
contract_cols = (((1,), (1,)), ((), ()))


def padded_2(x, sides, width):
    for axis, dim in sides:
        devices, length = (lax.axis_size(axis), x.shape[dim])
        up = [(i, (i + 1) % devices) for i in range(devices - 1)]
        down = [(j, i) for i, j in up]
        last = lax.slice_in_dim(x, length - width, length, axis=dim)
        leading = lax.slice_in_dim(x, 0, width, axis=dim)
        before = lax.ppermute(last, axis, up)
        after = lax.ppermute(leading, axis, down)
        x = jnp.concatenate([before, x, after], axis=dim)
    return x


def gelu_exact(values):
    return 0.5 * values * (1.0 + jax.scipy.special.erf(values * inv_root_two))


def gelu_slope(values):
    cdf_part = 0.5 * (1.0 + jax.scipy.special.erf(values * inv_root_two))
    return cdf_part + values * jnp.exp(-0.5 * values * values) * inv_root_two_pi


def small_sums(kernel_part, gain_part, scale_part, width):
    every = ("dp", "fsdp", "rows")
    devices = lax.axis_size(every)
    packed = jnp.concatenate(
        [kernel_part.reshape(KS * KS, width), gain_part[None], scale_part[None]], axis=0
    )
    count = packed.shape[0]
    per = -(-count // devices)
    packed = jnp.pad(packed, ((0, per * devices - count), (0, 0)))
    mine = lax.all_to_all(packed.reshape(devices, per, width), every, 0, 0, tiled=True).sum(0)
    spread = jnp.broadcast_to(mine[None], (devices, per, width))
    total = lax.all_to_all(spread, every, 0, 0, tiled=True).reshape(devices * per, width)
    kernel_sum = total[: KS * KS].reshape(KS, KS, width)
    return kernel_sum, total[KS * KS], total[KS * KS + 1]


def body(feature_maps, dw_kernel, norm_gain, w_up, w_down, layer_scale, d_out):
    scenes, strip, across, width = feature_maps.shape
    cells = scenes * strip * across
    hid_axes = ("fsdp", "rows")
    up_loc = lax.all_to_all(w_up, "rows", 1, 0, tiled=True)
    up_loc = lax.all_gather(up_loc, "dp", axis=0, tiled=True)
    down_loc = lax.all_to_all(w_down, "rows", 0, 1, tiled=True)
    down_loc = lax.all_gather(down_loc, "dp", axis=1, tiled=True)
    cotan = d_out.reshape(cells, width).astype(jnp.float32)
    back = (cotan * layer_scale).astype(jnp.bfloat16)
    back_all = lax.all_gather(back, hid_axes, axis=0, tiled=True)
    rimmed = padded_2(feature_maps, (("rows", 1),), 3)
    padded = jnp.pad(rimmed.astype(jnp.float32), ((0, 0), (0, 0), (3, 3), (0, 0)))
    filtered = jnp.zeros(feature_maps.shape, jnp.float32)
    for row_off in range(KS):
        for col_off in range(KS):
            filtered = (
                filtered
                + padded[:, row_off : row_off + strip, col_off : col_off + across, :]
                * dw_kernel[row_off, col_off]
            )
    flat = filtered.reshape(cells, width)
    average = jnp.mean(flat, axis=-1, keepdims=True)
    center = flat - average
    variance = jnp.mean(center * center, axis=-1, keepdims=True)
    rstd = lax.rsqrt(variance + norm_eps)
    normed = center * rstd
    scaled = (normed * norm_gain).astype(jnp.bfloat16)
    gathered = lax.all_gather(scaled, hid_axes, axis=0, tiled=True)
    hidden = jnp.dot(gathered, up_loc, preferred_element_type=jnp.float32)
    active = gelu_exact(hidden).astype(jnp.bfloat16)
    mlp_terms = jnp.dot(active, down_loc, preferred_element_type=jnp.float32)
    branch = lax.psum_scatter(
        mlp_terms.astype(jnp.bfloat16), hid_axes, scatter_dimension=0, tiled=True
    ).astype(jnp.float32)
    resid = feature_maps.reshape(cells, width).astype(jnp.float32)
    result = (resid + layer_scale * branch).astype(jnp.bfloat16).reshape(feature_maps.shape)
    scale_part = jnp.sum(cotan * branch, axis=0)
    down_part = lax.dot_general(active, back_all, contract_rows, preferred_element_type=jnp.float32)
    slope_in = lax.dot_general(
        back_all, down_loc, contract_cols, preferred_element_type=jnp.float32
    )
    hidden_grad = (slope_in * gelu_slope(hidden)).astype(jnp.bfloat16)
    up_part = lax.dot_general(
        gathered, hidden_grad, contract_rows, preferred_element_type=jnp.float32
    )
    norm_terms = lax.dot_general(
        hidden_grad, up_loc, contract_cols, preferred_element_type=jnp.float32
    )
    norm_grad = lax.psum_scatter(
        norm_terms.astype(jnp.bfloat16), hid_axes, scatter_dimension=0, tiled=True
    ).astype(jnp.float32)
    grad_up = lax.psum_scatter(
        up_part.astype(jnp.bfloat16), "dp", scatter_dimension=0, tiled=True
    )
    grad_up = lax.all_to_all(grad_up, "rows", 0, 1, tiled=True).astype(jnp.float32)
    grad_down = lax.psum_scatter(
        down_part.astype(jnp.bfloat16), "dp", scatter_dimension=1, tiled=True
    )
    grad_down = lax.all_to_all(grad_down, "rows", 1, 0, tiled=True).astype(jnp.float32)
    gain_part = jnp.sum(norm_grad * normed, axis=0)
    scaled_grad = norm_grad * norm_gain
    conv_grad = rstd * (
        scaled_grad
        - jnp.mean(scaled_grad, axis=-1, keepdims=True)
        - normed * jnp.mean(scaled_grad * normed, axis=-1, keepdims=True)
    )
    conv_grad = conv_grad.reshape(feature_maps.shape)
    grad_rim = padded_2(conv_grad.astype(jnp.bfloat16), (("rows", 1),), 3).astype(conv_grad.dtype)
    grad_pad = jnp.pad(grad_rim, ((0, 0), (0, 0), (3, 3), (0, 0)))
    kernel_rows = []
    back_conv = jnp.zeros(feature_maps.shape, jnp.float32)
    for row_off in range(KS):
        for col_off in range(KS):
            window = padded[:, row_off : row_off + strip, col_off : col_off + across, :]
            kernel_rows.append(jnp.sum(window * conv_grad, axis=(0, 1, 2)))
            back_conv = (
                back_conv
                + grad_pad[
                    :, 6 - row_off : 6 - row_off + strip, 6 - col_off : 6 - col_off + across, :
                ]
                * dw_kernel[row_off, col_off]
            )
    kernel_part = jnp.stack(kernel_rows).reshape(KS, KS, width)
    grad_x = (d_out.astype(jnp.float32) + back_conv).astype(jnp.bfloat16)
    grad_kernel, grad_gain, grad_scale = small_sums(kernel_part, gain_part, scale_part, width)
    return (result, grad_x, grad_up, grad_down, grad_kernel, grad_gain, grad_scale)


def solution(mesh):
    return jax.shard_map(
        body,
        mesh=mesh,
        in_specs=(
            P(("dp", "fsdp"), "rows", None, None),
            P(),
            P(),
            P(("dp", "rows"), "fsdp"),
            P("fsdp", ("dp", "rows")),
            P(),
            P(("dp", "fsdp"), "rows", None, None),
        ),
        out_specs=(
            P(("dp", "fsdp"), "rows", None, None),
            P(("dp", "fsdp"), "rows", None, None),
            P(("dp", "rows"), "fsdp"),
            P("fsdp", ("dp", "rows")),
            P(),
            P(),
            P(),
        ),
        check_vma=False,
    )
```

```python
import math

import jax
import jax.numpy as jnp
from jax import lax
from jax.sharding import PartitionSpec as P

KS = 7


norm_eps = 1e-06
inv_root_two = 1.0 / math.sqrt(2.0)
inv_root_two_pi = 1.0 / math.sqrt(2.0 * math.pi)
contract_rows = (((0,), (0,)), ((), ()))
contract_cols = (((1,), (1,)), ((), ()))


def padded_2(x, sides, width):
    for axis, dim in sides:
        devices, length = (lax.axis_size(axis), x.shape[dim])
        up = [(i, (i + 1) % devices) for i in range(devices - 1)]
        down = [(j, i) for i, j in up]
        last = lax.slice_in_dim(x, length - width, length, axis=dim)
        leading = lax.slice_in_dim(x, 0, width, axis=dim)
        before = lax.ppermute(last, axis, up)
        after = lax.ppermute(leading, axis, down)
        x = jnp.concatenate([before, x, after], axis=dim)
    return x


def gelu_exact(values):
    return 0.5 * values * (1.0 + jax.scipy.special.erf(values * inv_root_two))


def gelu_slope(values):
    cdf_part = 0.5 * (1.0 + jax.scipy.special.erf(values * inv_root_two))
    return cdf_part + values * jnp.exp(-0.5 * values * values) * inv_root_two_pi


def small_sums(kernel_part, gain_part, scale_part, width):
    every = ("dp", "fsdp", "rows")
    devices = lax.axis_size(every)
    packed = jnp.concatenate(
        [kernel_part.reshape(KS * KS, width), gain_part[None], scale_part[None]], axis=0
    )
    count = packed.shape[0]
    per = -(-count // devices)
    packed = jnp.pad(packed, ((0, per * devices - count), (0, 0)))
    mine = lax.all_to_all(packed.reshape(devices, per, width), every, 0, 0, tiled=True).sum(0)
    spread = jnp.broadcast_to(mine[None], (devices, per, width))
    total = lax.all_to_all(spread, every, 0, 0, tiled=True).reshape(devices * per, width)
    kernel_sum = total[: KS * KS].reshape(KS, KS, width)
    return kernel_sum, total[KS * KS], total[KS * KS + 1]


def shifts(devices):
    return [d for d in range(1, devices)] + [-d for d in range(1, devices)]


def line_perm(devices, d):
    return [(i, i + d) for i in range(devices) if 0 <= i + d < devices]


def gather_dp(x):
    devices = lax.axis_size("dp")
    me = lax.axis_index("dp")
    got = {d: lax.ppermute(x, "dp", line_perm(devices, d)) for d in shifts(devices)}
    order = [got[d] for d in range(devices - 1, 0, -1)] + [x] + [got[-d] for d in range(1, devices)]
    stacked = jnp.stack(order)
    return lax.dynamic_slice_in_dim(stacked, devices - 1 - me, devices, axis=0)


def scatter_sum_dp(parts):
    devices = lax.axis_size("dp")
    me = lax.axis_index("dp")
    sent = parts.astype(jnp.bfloat16)
    total = lax.dynamic_index_in_dim(parts, me, axis=0, keepdims=False)
    for d in shifts(devices):
        target = jnp.clip(me + d, 0, devices - 1)
        block = lax.dynamic_index_in_dim(sent, target, axis=0, keepdims=False)
        total = total + lax.ppermute(block, "dp", line_perm(devices, d)).astype(jnp.float32)
    return total


def body(feature_maps, dw_kernel, norm_gain, w_up, w_down, layer_scale, d_out):
    scenes, strip, across, width = feature_maps.shape
    cells = scenes * strip * across
    hid_axes = ("fsdp", "rows")
    up_loc = gather_dp(lax.all_to_all(w_up, "rows", 1, 0, tiled=True))
    dp_size, block_c, hid_part = up_loc.shape
    up_loc = up_loc.reshape(dp_size * block_c, hid_part)
    down3 = gather_dp(lax.all_to_all(w_down, "rows", 0, 1, tiled=True))
    cotan = d_out.reshape(cells, width).astype(jnp.float32)
    back = (cotan * layer_scale).astype(jnp.bfloat16)
    back_all = lax.all_gather(back, hid_axes, axis=0, tiled=True)
    rimmed = padded_2(feature_maps, (("rows", 1),), 3)
    padded = jnp.pad(rimmed.astype(jnp.float32), ((0, 0), (0, 0), (3, 3), (0, 0)))
    filtered = jnp.zeros(feature_maps.shape, jnp.float32)
    for row_off in range(KS):
        for col_off in range(KS):
            filtered = (
                filtered
                + padded[:, row_off : row_off + strip, col_off : col_off + across, :]
                * dw_kernel[row_off, col_off]
            )
    flat = filtered.reshape(cells, width)
    average = jnp.mean(flat, axis=-1, keepdims=True)
    center = flat - average
    variance = jnp.mean(center * center, axis=-1, keepdims=True)
    rstd = lax.rsqrt(variance + norm_eps)
    normed = center * rstd
    scaled = (normed * norm_gain).astype(jnp.bfloat16)
    gathered = lax.all_gather(scaled, hid_axes, axis=0, tiled=True)
    hidden = jnp.dot(gathered, up_loc, preferred_element_type=jnp.float32)
    active = gelu_exact(hidden).astype(jnp.bfloat16)
    mlp_terms = jnp.einsum(
        "xh,khj->xkj", active, down3, preferred_element_type=jnp.float32
    ).reshape(active.shape[0], width)
    branch = lax.psum_scatter(
        mlp_terms.astype(jnp.bfloat16), hid_axes, scatter_dimension=0, tiled=True
    ).astype(jnp.float32)
    resid = feature_maps.reshape(cells, width).astype(jnp.float32)
    result = (resid + layer_scale * branch).astype(jnp.bfloat16).reshape(feature_maps.shape)
    scale_part = jnp.sum(cotan * branch, axis=0)
    down_part_t = lax.dot_general(
        back_all, active, contract_rows, preferred_element_type=jnp.float32
    )
    slope_in = jnp.einsum(
        "xkj,khj->xh",
        back_all.reshape(back_all.shape[0], dp_size, block_c),
        down3,
        preferred_element_type=jnp.float32,
    )
    hidden_grad = (slope_in * gelu_slope(hidden)).astype(jnp.bfloat16)
    up_part = lax.dot_general(
        gathered, hidden_grad, contract_rows, preferred_element_type=jnp.float32
    )
    norm_terms = lax.dot_general(
        hidden_grad, up_loc, contract_cols, preferred_element_type=jnp.float32
    )
    norm_grad = lax.psum_scatter(
        norm_terms.astype(jnp.bfloat16), hid_axes, scatter_dimension=0, tiled=True
    ).astype(jnp.float32)
    grad_up = scatter_sum_dp(up_part.reshape(dp_size, block_c, hid_part))
    grad_up = lax.all_to_all(grad_up, "rows", 0, 1, tiled=True)
    grad_down_t = scatter_sum_dp(down_part_t.reshape(dp_size, block_c, hid_part))
    grad_down = lax.all_to_all(grad_down_t, "rows", 0, 1, tiled=True).T
    gain_part = jnp.sum(norm_grad * normed, axis=0)
    scaled_grad = norm_grad * norm_gain
    conv_grad = rstd * (
        scaled_grad
        - jnp.mean(scaled_grad, axis=-1, keepdims=True)
        - normed * jnp.mean(scaled_grad * normed, axis=-1, keepdims=True)
    )
    conv_grad = conv_grad.reshape(feature_maps.shape)
    grad_rim = padded_2(conv_grad.astype(jnp.bfloat16), (("rows", 1),), 3).astype(conv_grad.dtype)
    grad_pad = jnp.pad(grad_rim, ((0, 0), (0, 0), (3, 3), (0, 0)))
    kernel_rows = []
    back_conv = jnp.zeros(feature_maps.shape, jnp.float32)
    for row_off in range(KS):
        for col_off in range(KS):
            window = padded[:, row_off : row_off + strip, col_off : col_off + across, :]
            kernel_rows.append(jnp.sum(window * conv_grad, axis=(0, 1, 2)))
            back_conv = (
                back_conv
                + grad_pad[
                    :, 6 - row_off : 6 - row_off + strip, 6 - col_off : 6 - col_off + across, :
                ]
                * dw_kernel[row_off, col_off]
            )
    kernel_part = jnp.stack(kernel_rows).reshape(KS, KS, width)
    grad_x = (d_out.astype(jnp.float32) + back_conv).astype(jnp.bfloat16)
    grad_kernel, grad_gain, grad_scale = small_sums(kernel_part, gain_part, scale_part, width)
    return (result, grad_x, grad_up, grad_down, grad_kernel, grad_gain, grad_scale)


def solution(mesh):
    return jax.shard_map(
        body,
        mesh=mesh,
        in_specs=(
            P(("dp", "fsdp"), "rows", None, None),
            P(),
            P(),
            P(("dp", "rows"), "fsdp"),
            P("fsdp", ("dp", "rows")),
            P(),
            P(("dp", "fsdp"), "rows", None, None),
        ),
        out_specs=(
            P(("dp", "fsdp"), "rows", None, None),
            P(("dp", "fsdp"), "rows", None, None),
            P(("dp", "rows"), "fsdp"),
            P("fsdp", ("dp", "rows")),
            P(),
            P(),
            P(),
        ),
        check_vma=False,
    )
```

```python
import math

import jax
import jax.numpy as jnp
from jax import lax
from jax.sharding import PartitionSpec as P

KS = 7


norm_eps = 1e-06
inv_root_two = 1.0 / math.sqrt(2.0)
inv_root_two_pi = 1.0 / math.sqrt(2.0 * math.pi)
contract_rows = (((0,), (0,)), ((), ()))
contract_cols = (((1,), (1,)), ((), ()))


def padded_2(x, sides, width):
    for axis, dim in sides:
        devices, length = (lax.axis_size(axis), x.shape[dim])
        up = [(i, (i + 1) % devices) for i in range(devices - 1)]
        down = [(j, i) for i, j in up]
        last = lax.slice_in_dim(x, length - width, length, axis=dim)
        leading = lax.slice_in_dim(x, 0, width, axis=dim)
        before = lax.ppermute(last, axis, up)
        after = lax.ppermute(leading, axis, down)
        x = jnp.concatenate([before, x, after], axis=dim)
    return x


def gelu_exact(values):
    return 0.5 * values * (1.0 + jax.scipy.special.erf(values * inv_root_two))


def gelu_slope(values):
    cdf_part = 0.5 * (1.0 + jax.scipy.special.erf(values * inv_root_two))
    return cdf_part + values * jnp.exp(-0.5 * values * values) * inv_root_two_pi


def small_sums(kernel_part, gain_part, scale_part, width):
    every = ("dp", "fsdp", "rows")
    devices = lax.axis_size(every)
    packed = jnp.concatenate(
        [kernel_part.reshape(KS * KS, width), gain_part[None], scale_part[None]], axis=0
    )
    count = packed.shape[0]
    per = -(-count // devices)
    packed = jnp.pad(packed, ((0, per * devices - count), (0, 0)))
    mine = lax.all_to_all(packed.reshape(devices, per, width), every, 0, 0, tiled=True).sum(0)
    spread = jnp.broadcast_to(mine[None], (devices, per, width))
    total = lax.all_to_all(spread, every, 0, 0, tiled=True).reshape(devices * per, width)
    kernel_sum = total[: KS * KS].reshape(KS, KS, width)
    return kernel_sum, total[KS * KS], total[KS * KS + 1]


def body(feature_maps, dw_kernel, norm_gain, w_up, w_down, layer_scale, d_out):
    scenes, strip, across, width = feature_maps.shape
    cells = scenes * strip * across
    hid_axes = ("fsdp", "rows")
    up_mine = lax.all_to_all(w_up, "rows", 1, 0, tiled=True)
    down_mine = lax.all_to_all(w_down, "rows", 0, 1, tiled=True)
    both = lax.all_gather(jnp.stack([up_mine, down_mine.T]), "dp", axis=1, tiled=True)
    up_loc, down_t = both[0], both[1]
    cotan = d_out.reshape(cells, width).astype(jnp.float32)
    back = (cotan * layer_scale).astype(jnp.bfloat16)
    back_all = lax.all_gather(back, hid_axes, axis=0, tiled=True)
    rimmed = padded_2(feature_maps, (("rows", 1),), 3)
    padded = jnp.pad(rimmed.astype(jnp.float32), ((0, 0), (0, 0), (3, 3), (0, 0)))
    filtered = jnp.zeros(feature_maps.shape, jnp.float32)
    for row_off in range(KS):
        for col_off in range(KS):
            filtered = (
                filtered
                + padded[:, row_off : row_off + strip, col_off : col_off + across, :]
                * dw_kernel[row_off, col_off]
            )
    flat = filtered.reshape(cells, width)
    average = jnp.mean(flat, axis=-1, keepdims=True)
    center = flat - average
    variance = jnp.mean(center * center, axis=-1, keepdims=True)
    rstd = lax.rsqrt(variance + norm_eps)
    normed = center * rstd
    scaled = (normed * norm_gain).astype(jnp.bfloat16)
    gathered = lax.all_gather(scaled, hid_axes, axis=0, tiled=True)
    hidden = jnp.dot(gathered, up_loc, preferred_element_type=jnp.float32)
    active = gelu_exact(hidden).astype(jnp.bfloat16)
    mlp_terms = lax.dot_general(
        active, down_t, contract_cols, preferred_element_type=jnp.float32
    )
    branch = lax.psum_scatter(
        mlp_terms.astype(jnp.bfloat16), hid_axes, scatter_dimension=0, tiled=True
    ).astype(jnp.float32)
    resid = feature_maps.reshape(cells, width).astype(jnp.float32)
    result = (resid + layer_scale * branch).astype(jnp.bfloat16).reshape(feature_maps.shape)
    scale_part = jnp.sum(cotan * branch, axis=0)
    down_part_t = lax.dot_general(
        back_all, active, contract_rows, preferred_element_type=jnp.float32
    )
    slope_in = jnp.dot(back_all, down_t, preferred_element_type=jnp.float32)
    hidden_grad = (slope_in * gelu_slope(hidden)).astype(jnp.bfloat16)
    up_part = lax.dot_general(
        gathered, hidden_grad, contract_rows, preferred_element_type=jnp.float32
    )
    norm_terms = lax.dot_general(
        hidden_grad, up_loc, contract_cols, preferred_element_type=jnp.float32
    )
    norm_grad = lax.psum_scatter(
        norm_terms.astype(jnp.bfloat16), hid_axes, scatter_dimension=0, tiled=True
    ).astype(jnp.float32)
    dp_size = lax.axis_size("dp")
    grad_parts = jnp.stack([up_part, down_part_t]).astype(jnp.bfloat16)
    grad_parts = grad_parts.reshape(2, dp_size, -1, grad_parts.shape[-1])
    grad_sums = lax.all_to_all(grad_parts, "dp", 1, 1, tiled=True)
    grad_sums = grad_sums.astype(jnp.float32).sum(1)
    grad_up = lax.all_to_all(grad_sums[0], "rows", 0, 1, tiled=True)
    grad_down = lax.all_to_all(grad_sums[1], "rows", 0, 1, tiled=True).T
    gain_part = jnp.sum(norm_grad * normed, axis=0)
    scaled_grad = norm_grad * norm_gain
    conv_grad = rstd * (
        scaled_grad
        - jnp.mean(scaled_grad, axis=-1, keepdims=True)
        - normed * jnp.mean(scaled_grad * normed, axis=-1, keepdims=True)
    )
    conv_grad = conv_grad.reshape(feature_maps.shape)
    grad_rim = padded_2(conv_grad.astype(jnp.bfloat16), (("rows", 1),), 3).astype(conv_grad.dtype)
    grad_pad = jnp.pad(grad_rim, ((0, 0), (0, 0), (3, 3), (0, 0)))
    kernel_rows = []
    back_conv = jnp.zeros(feature_maps.shape, jnp.float32)
    for row_off in range(KS):
        for col_off in range(KS):
            window = padded[:, row_off : row_off + strip, col_off : col_off + across, :]
            kernel_rows.append(jnp.sum(window * conv_grad, axis=(0, 1, 2)))
            back_conv = (
                back_conv
                + grad_pad[
                    :, 6 - row_off : 6 - row_off + strip, 6 - col_off : 6 - col_off + across, :
                ]
                * dw_kernel[row_off, col_off]
            )
    kernel_part = jnp.stack(kernel_rows).reshape(KS, KS, width)
    grad_x = (d_out.astype(jnp.float32) + back_conv).astype(jnp.bfloat16)
    grad_kernel, grad_gain, grad_scale = small_sums(kernel_part, gain_part, scale_part, width)
    return (result, grad_x, grad_up, grad_down, grad_kernel, grad_gain, grad_scale)


def solution(mesh):
    return jax.shard_map(
        body,
        mesh=mesh,
        in_specs=(
            P(("dp", "fsdp"), "rows", None, None),
            P(),
            P(),
            P(("dp", "rows"), "fsdp"),
            P("fsdp", ("dp", "rows")),
            P(),
            P(("dp", "fsdp"), "rows", None, None),
        ),
        out_specs=(
            P(("dp", "fsdp"), "rows", None, None),
            P(("dp", "fsdp"), "rows", None, None),
            P(("dp", "rows"), "fsdp"),
            P("fsdp", ("dp", "rows")),
            P(),
            P(),
            P(),
        ),
        check_vma=False,
    )
```

```python
import math

import jax
import jax.numpy as jnp
from jax import lax
from jax.sharding import PartitionSpec as P

KS = 7


norm_eps = 1e-06
inv_root_two = 1.0 / math.sqrt(2.0)
inv_root_two_pi = 1.0 / math.sqrt(2.0 * math.pi)
contract_rows = (((0,), (0,)), ((), ()))
contract_cols = (((1,), (1,)), ((), ()))


def padded_2(x, sides, width):
    for axis, dim in sides:
        devices, length = (lax.axis_size(axis), x.shape[dim])
        up = [(i, (i + 1) % devices) for i in range(devices - 1)]
        down = [(j, i) for i, j in up]
        last = lax.slice_in_dim(x, length - width, length, axis=dim)
        leading = lax.slice_in_dim(x, 0, width, axis=dim)
        before = lax.ppermute(last, axis, up)
        after = lax.ppermute(leading, axis, down)
        x = jnp.concatenate([before, x, after], axis=dim)
    return x


def gelu_exact(values):
    return 0.5 * values * (1.0 + jax.scipy.special.erf(values * inv_root_two))


def gelu_slope(values):
    cdf_part = 0.5 * (1.0 + jax.scipy.special.erf(values * inv_root_two))
    return cdf_part + values * jnp.exp(-0.5 * values * values) * inv_root_two_pi


def small_sums(kernel_part, gain_part, scale_part, width):
    every = ("dp", "fsdp", "rows")
    devices = lax.axis_size(every)
    packed = jnp.concatenate(
        [kernel_part.reshape(KS * KS, width), gain_part[None], scale_part[None]], axis=0
    )
    count = packed.shape[0]
    per = -(-count // devices)
    packed = jnp.pad(packed, ((0, per * devices - count), (0, 0)))
    mine = lax.all_to_all(packed.reshape(devices, per, width), every, 0, 0, tiled=True).sum(0)
    spread = jnp.broadcast_to(mine[None], (devices, per, width))
    total = lax.all_to_all(spread, every, 0, 0, tiled=True).reshape(devices * per, width)
    kernel_sum = total[: KS * KS].reshape(KS, KS, width)
    return kernel_sum, total[KS * KS], total[KS * KS + 1]


def body(feature_maps, dw_kernel, norm_gain, w_up, w_down, layer_scale, d_out):
    scenes, strip, across, width = feature_maps.shape
    cells = scenes * strip * across
    hid_axes = ("fsdp", "rows")
    up_mine = lax.all_to_all(w_up, "rows", 1, 0, tiled=True)
    down_mine = lax.all_to_all(w_down, "rows", 0, 1, tiled=True)
    both = lax.all_gather(jnp.stack([up_mine, down_mine.T]), "dp", axis=1, tiled=True)
    up_loc, down_t = both[0], both[1]
    cotan = d_out.reshape(cells, width).astype(jnp.float32)
    back = (cotan * layer_scale).astype(jnp.bfloat16)
    back_all = lax.all_gather(back, hid_axes, axis=0, tiled=True)
    rimmed = padded_2(feature_maps, (("rows", 1),), 3)
    padded = jnp.pad(rimmed.astype(jnp.float32), ((0, 0), (0, 0), (3, 3), (0, 0)))
    filtered = jnp.zeros(feature_maps.shape, jnp.float32)
    for row_off in range(KS):
        for col_off in range(KS):
            filtered = (
                filtered
                + padded[:, row_off : row_off + strip, col_off : col_off + across, :]
                * dw_kernel[row_off, col_off]
            )
    flat = filtered.reshape(cells, width)
    average = jnp.mean(flat, axis=-1, keepdims=True)
    center = flat - average
    variance = jnp.mean(center * center, axis=-1, keepdims=True)
    rstd = lax.rsqrt(variance + norm_eps)
    normed = center * rstd
    scaled = (normed * norm_gain).astype(jnp.bfloat16)
    gathered = lax.all_gather(scaled, hid_axes, axis=0, tiled=True)
    hidden = jnp.dot(gathered, up_loc, preferred_element_type=jnp.float32)
    active = gelu_exact(hidden).astype(jnp.bfloat16)
    mlp_terms = lax.dot_general(
        active, down_t, contract_cols, preferred_element_type=jnp.float32
    )
    branch = lax.psum_scatter(
        mlp_terms.astype(jnp.bfloat16), hid_axes, scatter_dimension=0, tiled=True
    ).astype(jnp.float32)
    resid = feature_maps.reshape(cells, width).astype(jnp.float32)
    result = (resid + layer_scale * branch).astype(jnp.bfloat16).reshape(feature_maps.shape)
    scale_part = jnp.sum(cotan * branch, axis=0)
    down_part_t = lax.dot_general(
        back_all, active, contract_rows, preferred_element_type=jnp.float32
    )
    slope_in = jnp.dot(back_all, down_t, preferred_element_type=jnp.float32)
    hidden_grad = (slope_in * gelu_slope(hidden)).astype(jnp.bfloat16)
    up_part = lax.dot_general(
        gathered, hidden_grad, contract_rows, preferred_element_type=jnp.float32
    )
    norm_terms = lax.dot_general(
        hidden_grad, up_loc, contract_cols, preferred_element_type=jnp.float32
    )
    norm_grad = lax.psum_scatter(
        norm_terms.astype(jnp.bfloat16), hid_axes, scatter_dimension=0, tiled=True
    ).astype(jnp.float32)
    grad_parts = jnp.stack([up_part, down_part_t]).astype(jnp.bfloat16)
    grad_sums = lax.psum_scatter(grad_parts, "dp", scatter_dimension=1, tiled=True)
    grad_up = lax.all_to_all(grad_sums[0], "rows", 0, 1, tiled=True).astype(jnp.float32)
    grad_down = lax.all_to_all(grad_sums[1], "rows", 0, 1, tiled=True).T.astype(jnp.float32)
    gain_part = jnp.sum(norm_grad * normed, axis=0)
    scaled_grad = norm_grad * norm_gain
    conv_grad = rstd * (
        scaled_grad
        - jnp.mean(scaled_grad, axis=-1, keepdims=True)
        - normed * jnp.mean(scaled_grad * normed, axis=-1, keepdims=True)
    )
    conv_grad = conv_grad.reshape(feature_maps.shape)
    grad_rim = padded_2(conv_grad.astype(jnp.bfloat16), (("rows", 1),), 3).astype(conv_grad.dtype)
    grad_pad = jnp.pad(grad_rim, ((0, 0), (0, 0), (3, 3), (0, 0)))
    kernel_rows = []
    back_conv = jnp.zeros(feature_maps.shape, jnp.float32)
    for row_off in range(KS):
        for col_off in range(KS):
            window = padded[:, row_off : row_off + strip, col_off : col_off + across, :]
            kernel_rows.append(jnp.sum(window * conv_grad, axis=(0, 1, 2)))
            back_conv = (
                back_conv
                + grad_pad[
                    :, 6 - row_off : 6 - row_off + strip, 6 - col_off : 6 - col_off + across, :
                ]
                * dw_kernel[row_off, col_off]
            )
    kernel_part = jnp.stack(kernel_rows).reshape(KS, KS, width)
    grad_x = (d_out.astype(jnp.float32) + back_conv).astype(jnp.bfloat16)
    grad_kernel, grad_gain, grad_scale = small_sums(kernel_part, gain_part, scale_part, width)
    return (result, grad_x, grad_up, grad_down, grad_kernel, grad_gain, grad_scale)


def solution(mesh):
    return jax.shard_map(
        body,
        mesh=mesh,
        in_specs=(
            P(("dp", "fsdp"), "rows", None, None),
            P(),
            P(),
            P(("dp", "rows"), "fsdp"),
            P("fsdp", ("dp", "rows")),
            P(),
            P(("dp", "fsdp"), "rows", None, None),
        ),
        out_specs=(
            P(("dp", "fsdp"), "rows", None, None),
            P(("dp", "fsdp"), "rows", None, None),
            P(("dp", "rows"), "fsdp"),
            P("fsdp", ("dp", "rows")),
            P(),
            P(),
            P(),
        ),
        check_vma=False,
    )
```

```python
import math

import jax
import jax.numpy as jnp
from jax import lax
from jax.sharding import PartitionSpec as P

KS = 7


norm_eps = 1e-06
inv_root_two = 1.0 / math.sqrt(2.0)
inv_root_two_pi = 1.0 / math.sqrt(2.0 * math.pi)
contract_rows = (((0,), (0,)), ((), ()))
contract_cols = (((1,), (1,)), ((), ()))


def padded_2(x, sides, width):
    for axis, dim in sides:
        devices, length = (lax.axis_size(axis), x.shape[dim])
        up = [(i, (i + 1) % devices) for i in range(devices - 1)]
        down = [(j, i) for i, j in up]
        last = lax.slice_in_dim(x, length - width, length, axis=dim)
        leading = lax.slice_in_dim(x, 0, width, axis=dim)
        before = lax.ppermute(last, axis, up)
        after = lax.ppermute(leading, axis, down)
        x = jnp.concatenate([before, x, after], axis=dim)
    return x


def gelu_exact(values):
    return 0.5 * values * (1.0 + jax.scipy.special.erf(values * inv_root_two))


def gelu_slope(values):
    cdf_part = 0.5 * (1.0 + jax.scipy.special.erf(values * inv_root_two))
    return cdf_part + values * jnp.exp(-0.5 * values * values) * inv_root_two_pi


def small_sums(kernel_part, gain_part, scale_part, width):
    every = ("dp", "fsdp", "rows")
    devices = lax.axis_size(every)
    packed = jnp.concatenate(
        [kernel_part.reshape(KS * KS, width), gain_part[None], scale_part[None]], axis=0
    )
    count = packed.shape[0]
    per = -(-count // devices)
    packed = jnp.pad(packed, ((0, per * devices - count), (0, 0)))
    mine = lax.all_to_all(packed.reshape(devices, per, width), every, 0, 0, tiled=True).sum(0)
    spread = jnp.broadcast_to(mine[None], (devices, per, width))
    total = lax.all_to_all(spread, every, 0, 0, tiled=True).reshape(devices * per, width)
    kernel_sum = total[: KS * KS].reshape(KS, KS, width)
    return kernel_sum, total[KS * KS], total[KS * KS + 1]


def body(feature_maps, dw_kernel, norm_gain, w_up, w_down, layer_scale, d_out):
    scenes, strip, across, width = feature_maps.shape
    cells = scenes * strip * across
    hid_axes = ("fsdp", "rows")
    dp_size, row_size = lax.axis_size("dp"), lax.axis_size("rows")
    block_c, hid_f = w_up.shape
    both = lax.all_gather(jnp.stack([w_up, w_down.T]), "dp", axis=1, tiled=True)
    both = lax.all_to_all(both, "rows", 2, 1, tiled=True)
    both = both.reshape(2, row_size, dp_size, block_c, hid_f // row_size)
    both = both.transpose(0, 2, 1, 3, 4).reshape(2, dp_size * row_size * block_c, hid_f // row_size)
    up_loc, down_t = both[0], both[1]
    cotan = d_out.reshape(cells, width).astype(jnp.float32)
    back = (cotan * layer_scale).astype(jnp.bfloat16)
    back_all = lax.all_gather(back, hid_axes, axis=0, tiled=True)
    rimmed = padded_2(feature_maps, (("rows", 1),), 3)
    padded = jnp.pad(rimmed.astype(jnp.float32), ((0, 0), (0, 0), (3, 3), (0, 0)))
    filtered = jnp.zeros(feature_maps.shape, jnp.float32)
    for row_off in range(KS):
        for col_off in range(KS):
            filtered = (
                filtered
                + padded[:, row_off : row_off + strip, col_off : col_off + across, :]
                * dw_kernel[row_off, col_off]
            )
    flat = filtered.reshape(cells, width)
    average = jnp.mean(flat, axis=-1, keepdims=True)
    center = flat - average
    variance = jnp.mean(center * center, axis=-1, keepdims=True)
    rstd = lax.rsqrt(variance + norm_eps)
    normed = center * rstd
    scaled = (normed * norm_gain).astype(jnp.bfloat16)
    gathered = lax.all_gather(scaled, hid_axes, axis=0, tiled=True)
    hidden = jnp.dot(gathered, up_loc, preferred_element_type=jnp.float32)
    active = gelu_exact(hidden).astype(jnp.bfloat16)
    mlp_terms = lax.dot_general(
        active, down_t, contract_cols, preferred_element_type=jnp.float32
    )
    branch = lax.psum_scatter(
        mlp_terms.astype(jnp.bfloat16), hid_axes, scatter_dimension=0, tiled=True
    ).astype(jnp.float32)
    resid = feature_maps.reshape(cells, width).astype(jnp.float32)
    result = (resid + layer_scale * branch).astype(jnp.bfloat16).reshape(feature_maps.shape)
    scale_part = jnp.sum(cotan * branch, axis=0)
    down_part_t = lax.dot_general(
        back_all, active, contract_rows, preferred_element_type=jnp.float32
    )
    slope_in = jnp.dot(back_all, down_t, preferred_element_type=jnp.float32)
    hidden_grad = (slope_in * gelu_slope(hidden)).astype(jnp.bfloat16)
    up_part = lax.dot_general(
        gathered, hidden_grad, contract_rows, preferred_element_type=jnp.float32
    )
    norm_terms = lax.dot_general(
        hidden_grad, up_loc, contract_cols, preferred_element_type=jnp.float32
    )
    norm_grad = lax.psum_scatter(
        norm_terms.astype(jnp.bfloat16), hid_axes, scatter_dimension=0, tiled=True
    ).astype(jnp.float32)
    grad_parts = jnp.stack([up_part, down_part_t]).astype(jnp.bfloat16)
    grad_sums = lax.psum_scatter(grad_parts, "dp", scatter_dimension=1, tiled=True)
    grad_up = lax.all_to_all(grad_sums[0], "rows", 0, 1, tiled=True).astype(jnp.float32)
    grad_down = lax.all_to_all(grad_sums[1], "rows", 0, 1, tiled=True).T.astype(jnp.float32)
    gain_part = jnp.sum(norm_grad * normed, axis=0)
    scaled_grad = norm_grad * norm_gain
    conv_grad = rstd * (
        scaled_grad
        - jnp.mean(scaled_grad, axis=-1, keepdims=True)
        - normed * jnp.mean(scaled_grad * normed, axis=-1, keepdims=True)
    )
    conv_grad = conv_grad.reshape(feature_maps.shape)
    grad_rim = padded_2(conv_grad.astype(jnp.bfloat16), (("rows", 1),), 3).astype(conv_grad.dtype)
    grad_pad = jnp.pad(grad_rim, ((0, 0), (0, 0), (3, 3), (0, 0)))
    kernel_rows = []
    back_conv = jnp.zeros(feature_maps.shape, jnp.float32)
    for row_off in range(KS):
        for col_off in range(KS):
            window = padded[:, row_off : row_off + strip, col_off : col_off + across, :]
            kernel_rows.append(jnp.sum(window * conv_grad, axis=(0, 1, 2)))
            back_conv = (
                back_conv
                + grad_pad[
                    :, 6 - row_off : 6 - row_off + strip, 6 - col_off : 6 - col_off + across, :
                ]
                * dw_kernel[row_off, col_off]
            )
    kernel_part = jnp.stack(kernel_rows).reshape(KS, KS, width)
    grad_x = (d_out.astype(jnp.float32) + back_conv).astype(jnp.bfloat16)
    grad_kernel, grad_gain, grad_scale = small_sums(kernel_part, gain_part, scale_part, width)
    return (result, grad_x, grad_up, grad_down, grad_kernel, grad_gain, grad_scale)


def solution(mesh):
    return jax.shard_map(
        body,
        mesh=mesh,
        in_specs=(
            P(("dp", "fsdp"), "rows", None, None),
            P(),
            P(),
            P(("dp", "rows"), "fsdp"),
            P("fsdp", ("dp", "rows")),
            P(),
            P(("dp", "fsdp"), "rows", None, None),
        ),
        out_specs=(
            P(("dp", "fsdp"), "rows", None, None),
            P(("dp", "fsdp"), "rows", None, None),
            P(("dp", "rows"), "fsdp"),
            P("fsdp", ("dp", "rows")),
            P(),
            P(),
            P(),
        ),
        check_vma=False,
    )
```

```python
import math

import jax
import jax.numpy as jnp
from jax import lax
from jax.sharding import PartitionSpec as P

KS = 7


norm_eps = 1e-06
inv_root_two = 1.0 / math.sqrt(2.0)
inv_root_two_pi = 1.0 / math.sqrt(2.0 * math.pi)
contract_rows = (((0,), (0,)), ((), ()))
contract_cols = (((1,), (1,)), ((), ()))


def padded_2(x, sides, width):
    for axis, dim in sides:
        devices, length = (lax.axis_size(axis), x.shape[dim])
        up = [(i, (i + 1) % devices) for i in range(devices - 1)]
        down = [(j, i) for i, j in up]
        last = lax.slice_in_dim(x, length - width, length, axis=dim)
        leading = lax.slice_in_dim(x, 0, width, axis=dim)
        before = lax.ppermute(last, axis, up)
        after = lax.ppermute(leading, axis, down)
        x = jnp.concatenate([before, x, after], axis=dim)
    return x


def gelu_exact(values):
    return 0.5 * values * (1.0 + jax.scipy.special.erf(values * inv_root_two))


def gelu_slope(values):
    cdf_part = 0.5 * (1.0 + jax.scipy.special.erf(values * inv_root_two))
    return cdf_part + values * jnp.exp(-0.5 * values * values) * inv_root_two_pi


def small_sums(kernel_part, gain_part, scale_part, width):
    every = ("dp", "fsdp", "rows")
    devices = lax.axis_size(every)
    packed = jnp.concatenate(
        [kernel_part.reshape(KS * KS, width), gain_part[None], scale_part[None]], axis=0
    )
    count = packed.shape[0]
    per = -(-count // devices)
    packed = jnp.pad(packed, ((0, per * devices - count), (0, 0)))
    mine = lax.all_to_all(packed.reshape(devices, per, width), every, 0, 0, tiled=True).sum(0)
    spread = jnp.broadcast_to(mine[None], (devices, per, width))
    total = lax.all_to_all(spread, every, 0, 0, tiled=True).reshape(devices * per, width)
    kernel_sum = total[: KS * KS].reshape(KS, KS, width)
    return kernel_sum, total[KS * KS], total[KS * KS + 1]


def body(feature_maps, dw_kernel, norm_gain, w_up, w_down, layer_scale, d_out):
    scenes, strip, across, width = feature_maps.shape
    cells = scenes * strip * across
    hid_axes = ("fsdp", "rows")
    up_loc = lax.all_to_all(w_up, "rows", 1, 0, tiled=True)
    up_loc = lax.all_gather(up_loc, "dp", axis=0, tiled=True)
    down_loc = lax.all_to_all(w_down, "rows", 0, 1, tiled=True)
    down_loc = lax.all_gather(down_loc, "dp", axis=1, tiled=True)
    cotan = d_out.reshape(cells, width).astype(jnp.float32)
    back = (cotan * layer_scale).astype(jnp.bfloat16)
    rimmed = padded_2(feature_maps, (("rows", 1),), 3)
    padded = jnp.pad(rimmed.astype(jnp.float32), ((0, 0), (0, 0), (3, 3), (0, 0)))
    filtered = jnp.zeros(feature_maps.shape, jnp.float32)
    for row_off in range(KS):
        for col_off in range(KS):
            filtered = (
                filtered
                + padded[:, row_off : row_off + strip, col_off : col_off + across, :]
                * dw_kernel[row_off, col_off]
            )
    flat = filtered.reshape(cells, width)
    average = jnp.mean(flat, axis=-1, keepdims=True)
    center = flat - average
    variance = jnp.mean(center * center, axis=-1, keepdims=True)
    rstd = lax.rsqrt(variance + norm_eps)
    normed = center * rstd
    scaled = (normed * norm_gain).astype(jnp.bfloat16)
    pair = lax.all_gather(jnp.stack([scaled, back]), hid_axes, axis=1, tiled=True)
    gathered, back_all = pair[0], pair[1]
    hidden = jnp.dot(gathered, up_loc, preferred_element_type=jnp.float32)
    active = gelu_exact(hidden).astype(jnp.bfloat16)
    mlp_terms = jnp.dot(active, down_loc, preferred_element_type=jnp.float32)
    branch = lax.psum_scatter(
        mlp_terms.astype(jnp.bfloat16), hid_axes, scatter_dimension=0, tiled=True
    ).astype(jnp.float32)
    resid = feature_maps.reshape(cells, width).astype(jnp.float32)
    result = (resid + layer_scale * branch).astype(jnp.bfloat16).reshape(feature_maps.shape)
    scale_part = jnp.sum(cotan * branch, axis=0)
    down_part_t = lax.dot_general(
        back_all, active, contract_rows, preferred_element_type=jnp.float32
    )
    slope_in = lax.dot_general(
        back_all, down_loc, contract_cols, preferred_element_type=jnp.float32
    )
    hidden_grad = (slope_in * gelu_slope(hidden)).astype(jnp.bfloat16)
    up_part = lax.dot_general(
        gathered, hidden_grad, contract_rows, preferred_element_type=jnp.float32
    )
    norm_terms = lax.dot_general(
        hidden_grad, up_loc, contract_cols, preferred_element_type=jnp.float32
    )
    norm_grad = lax.psum_scatter(
        norm_terms.astype(jnp.bfloat16), hid_axes, scatter_dimension=0, tiled=True
    ).astype(jnp.float32)
    grad_parts = jnp.stack([up_part, down_part_t]).astype(jnp.bfloat16)
    grad_sums = lax.psum_scatter(grad_parts, "dp", scatter_dimension=1, tiled=True)
    grad_up = lax.all_to_all(grad_sums[0], "rows", 0, 1, tiled=True).astype(jnp.float32)
    grad_down = lax.all_to_all(grad_sums[1], "rows", 0, 1, tiled=True).T.astype(jnp.float32)
    gain_part = jnp.sum(norm_grad * normed, axis=0)
    scaled_grad = norm_grad * norm_gain
    conv_grad = rstd * (
        scaled_grad
        - jnp.mean(scaled_grad, axis=-1, keepdims=True)
        - normed * jnp.mean(scaled_grad * normed, axis=-1, keepdims=True)
    )
    conv_grad = conv_grad.reshape(feature_maps.shape)
    grad_rim = padded_2(conv_grad.astype(jnp.bfloat16), (("rows", 1),), 3).astype(conv_grad.dtype)
    grad_pad = jnp.pad(grad_rim, ((0, 0), (0, 0), (3, 3), (0, 0)))
    kernel_rows = []
    back_conv = jnp.zeros(feature_maps.shape, jnp.float32)
    for row_off in range(KS):
        for col_off in range(KS):
            window = padded[:, row_off : row_off + strip, col_off : col_off + across, :]
            kernel_rows.append(jnp.sum(window * conv_grad, axis=(0, 1, 2)))
            back_conv = (
                back_conv
                + grad_pad[
                    :, 6 - row_off : 6 - row_off + strip, 6 - col_off : 6 - col_off + across, :
                ]
                * dw_kernel[row_off, col_off]
            )
    kernel_part = jnp.stack(kernel_rows).reshape(KS, KS, width)
    grad_x = (d_out.astype(jnp.float32) + back_conv).astype(jnp.bfloat16)
    grad_kernel, grad_gain, grad_scale = small_sums(kernel_part, gain_part, scale_part, width)
    return (result, grad_x, grad_up, grad_down, grad_kernel, grad_gain, grad_scale)


def solution(mesh):
    return jax.shard_map(
        body,
        mesh=mesh,
        in_specs=(
            P(("dp", "fsdp"), "rows", None, None),
            P(),
            P(),
            P(("dp", "rows"), "fsdp"),
            P("fsdp", ("dp", "rows")),
            P(),
            P(("dp", "fsdp"), "rows", None, None),
        ),
        out_specs=(
            P(("dp", "fsdp"), "rows", None, None),
            P(("dp", "fsdp"), "rows", None, None),
            P(("dp", "rows"), "fsdp"),
            P("fsdp", ("dp", "rows")),
            P(),
            P(),
            P(),
        ),
        check_vma=False,
    )
```

```python
import math

import jax
import jax.numpy as jnp
from jax import lax
from jax.sharding import PartitionSpec as P

KS = 7


norm_eps = 1e-06
inv_root_two = 1.0 / math.sqrt(2.0)
inv_root_two_pi = 1.0 / math.sqrt(2.0 * math.pi)
contract_rows = (((0,), (0,)), ((), ()))
contract_cols = (((1,), (1,)), ((), ()))


def padded_2(x, sides, width):
    for axis, dim in sides:
        devices, length = (lax.axis_size(axis), x.shape[dim])
        up = [(i, (i + 1) % devices) for i in range(devices - 1)]
        down = [(j, i) for i, j in up]
        last = lax.slice_in_dim(x, length - width, length, axis=dim)
        leading = lax.slice_in_dim(x, 0, width, axis=dim)
        before = lax.ppermute(last, axis, up)
        after = lax.ppermute(leading, axis, down)
        x = jnp.concatenate([before, x, after], axis=dim)
    return x


def gelu_exact(values):
    return 0.5 * values * (1.0 + jax.scipy.special.erf(values * inv_root_two))


def gelu_slope(values):
    cdf_part = 0.5 * (1.0 + jax.scipy.special.erf(values * inv_root_two))
    return cdf_part + values * jnp.exp(-0.5 * values * values) * inv_root_two_pi


def small_sums(kernel_part, gain_part, scale_part, width):
    every = ("dp", "fsdp", "rows")
    devices = lax.axis_size(every)
    packed = jnp.concatenate(
        [kernel_part.reshape(KS * KS, width), gain_part[None], scale_part[None]], axis=0
    )
    count = packed.shape[0]
    per = -(-count // devices)
    packed = jnp.pad(packed, ((0, per * devices - count), (0, 0)))
    mine = lax.all_to_all(packed.reshape(devices, per, width), every, 0, 0, tiled=True).sum(0)
    spread = jnp.broadcast_to(mine[None], (devices, per, width))
    total = lax.all_to_all(spread, every, 0, 0, tiled=True).reshape(devices * per, width)
    kernel_sum = total[: KS * KS].reshape(KS, KS, width)
    return kernel_sum, total[KS * KS], total[KS * KS + 1]


def body(feature_maps, dw_kernel, norm_gain, w_up, w_down, layer_scale, d_out):
    scenes, strip, across, width = feature_maps.shape
    cells = scenes * strip * across
    hid_axes = ("fsdp", "rows")
    up_mine = lax.all_to_all(w_up, "rows", 1, 0, tiled=True)
    down_mine = lax.all_to_all(w_down, "rows", 0, 1, tiled=True)
    both = lax.all_gather(jnp.stack([up_mine, down_mine.T]), "dp", axis=1, tiled=True)
    up_loc, down_t = both[0], both[1]
    cotan = d_out.reshape(cells, width).astype(jnp.float32)
    back = (cotan * layer_scale).astype(jnp.bfloat16)
    rimmed = padded_2(feature_maps, (("rows", 1),), 3)
    padded = jnp.pad(rimmed.astype(jnp.float32), ((0, 0), (0, 0), (3, 3), (0, 0)))
    filtered = jnp.zeros(feature_maps.shape, jnp.float32)
    for row_off in range(KS):
        for col_off in range(KS):
            filtered = (
                filtered
                + padded[:, row_off : row_off + strip, col_off : col_off + across, :]
                * dw_kernel[row_off, col_off]
            )
    flat = filtered.reshape(cells, width)
    average = jnp.mean(flat, axis=-1, keepdims=True)
    center = flat - average
    variance = jnp.mean(center * center, axis=-1, keepdims=True)
    rstd = lax.rsqrt(variance + norm_eps)
    normed = center * rstd
    scaled = (normed * norm_gain).astype(jnp.bfloat16)
    pair = lax.all_gather(jnp.stack([scaled, back]), hid_axes, axis=1, tiled=True)
    gathered, back_all = pair[0], pair[1]
    hidden = jnp.dot(gathered, up_loc, preferred_element_type=jnp.float32)
    active = gelu_exact(hidden).astype(jnp.bfloat16)
    mlp_terms = lax.dot_general(
        active, down_t, contract_cols, preferred_element_type=jnp.float32
    )
    down_part_t = lax.dot_general(
        back_all, active, contract_rows, preferred_element_type=jnp.float32
    )
    slope_in = jnp.dot(back_all, down_t, preferred_element_type=jnp.float32)
    hidden_grad = (slope_in * gelu_slope(hidden)).astype(jnp.bfloat16)
    up_part = lax.dot_general(
        gathered, hidden_grad, contract_rows, preferred_element_type=jnp.float32
    )
    norm_terms = lax.dot_general(
        hidden_grad, up_loc, contract_cols, preferred_element_type=jnp.float32
    )
    sums = lax.psum_scatter(
        jnp.stack([mlp_terms, norm_terms]).astype(jnp.bfloat16),
        hid_axes,
        scatter_dimension=1,
        tiled=True,
    ).astype(jnp.float32)
    branch, norm_grad = sums[0], sums[1]
    resid = feature_maps.reshape(cells, width).astype(jnp.float32)
    result = (resid + layer_scale * branch).astype(jnp.bfloat16).reshape(feature_maps.shape)
    scale_part = jnp.sum(cotan * branch, axis=0)
    grad_parts = jnp.stack([up_part, down_part_t]).astype(jnp.bfloat16)
    grad_sums = lax.psum_scatter(grad_parts, "dp", scatter_dimension=1, tiled=True)
    grad_up = lax.all_to_all(grad_sums[0], "rows", 0, 1, tiled=True).astype(jnp.float32)
    grad_down = lax.all_to_all(grad_sums[1], "rows", 0, 1, tiled=True).T.astype(jnp.float32)
    gain_part = jnp.sum(norm_grad * normed, axis=0)
    scaled_grad = norm_grad * norm_gain
    conv_grad = rstd * (
        scaled_grad
        - jnp.mean(scaled_grad, axis=-1, keepdims=True)
        - normed * jnp.mean(scaled_grad * normed, axis=-1, keepdims=True)
    )
    conv_grad = conv_grad.reshape(feature_maps.shape)
    grad_rim = padded_2(conv_grad.astype(jnp.bfloat16), (("rows", 1),), 3).astype(conv_grad.dtype)
    grad_pad = jnp.pad(grad_rim, ((0, 0), (0, 0), (3, 3), (0, 0)))
    kernel_rows = []
    back_conv = jnp.zeros(feature_maps.shape, jnp.float32)
    for row_off in range(KS):
        for col_off in range(KS):
            window = padded[:, row_off : row_off + strip, col_off : col_off + across, :]
            kernel_rows.append(jnp.sum(window * conv_grad, axis=(0, 1, 2)))
            back_conv = (
                back_conv
                + grad_pad[
                    :, 6 - row_off : 6 - row_off + strip, 6 - col_off : 6 - col_off + across, :
                ]
                * dw_kernel[row_off, col_off]
            )
    kernel_part = jnp.stack(kernel_rows).reshape(KS, KS, width)
    grad_x = (d_out.astype(jnp.float32) + back_conv).astype(jnp.bfloat16)
    grad_kernel, grad_gain, grad_scale = small_sums(kernel_part, gain_part, scale_part, width)
    return (result, grad_x, grad_up, grad_down, grad_kernel, grad_gain, grad_scale)


def solution(mesh):
    return jax.shard_map(
        body,
        mesh=mesh,
        in_specs=(
            P(("dp", "fsdp"), "rows", None, None),
            P(),
            P(),
            P(("dp", "rows"), "fsdp"),
            P("fsdp", ("dp", "rows")),
            P(),
            P(("dp", "fsdp"), "rows", None, None),
        ),
        out_specs=(
            P(("dp", "fsdp"), "rows", None, None),
            P(("dp", "fsdp"), "rows", None, None),
            P(("dp", "rows"), "fsdp"),
            P("fsdp", ("dp", "rows")),
            P(),
            P(),
            P(),
        ),
        check_vma=False,
    )
```

```python
import math

import jax
import jax.numpy as jnp
from jax import lax
from jax.sharding import PartitionSpec as P

KS = 7


norm_eps = 1e-06
inv_root_two = 1.0 / math.sqrt(2.0)
inv_root_two_pi = 1.0 / math.sqrt(2.0 * math.pi)
contract_rows = (((0,), (0,)), ((), ()))
contract_cols = (((1,), (1,)), ((), ()))


def padded_2(x, sides, width):
    for axis, dim in sides:
        devices, length = (lax.axis_size(axis), x.shape[dim])
        up = [(i, (i + 1) % devices) for i in range(devices - 1)]
        down = [(j, i) for i, j in up]
        last = lax.slice_in_dim(x, length - width, length, axis=dim)
        leading = lax.slice_in_dim(x, 0, width, axis=dim)
        before = lax.ppermute(last, axis, up)
        after = lax.ppermute(leading, axis, down)
        x = jnp.concatenate([before, x, after], axis=dim)
    return x


def gelu_exact(values):
    return 0.5 * values * (1.0 + jax.scipy.special.erf(values * inv_root_two))


def gelu_slope(values):
    cdf_part = 0.5 * (1.0 + jax.scipy.special.erf(values * inv_root_two))
    return cdf_part + values * jnp.exp(-0.5 * values * values) * inv_root_two_pi


def small_sums(kernel_part, gain_part, scale_part, width):
    every = ("dp", "fsdp", "rows")
    devices = lax.axis_size(every)
    packed = jnp.concatenate(
        [kernel_part.reshape(KS * KS, width), gain_part[None], scale_part[None]], axis=0
    )
    count = packed.shape[0]
    per = -(-count // devices)
    packed = jnp.pad(packed, ((0, per * devices - count), (0, 0)))
    mine = lax.all_to_all(packed.reshape(devices, per, width), every, 0, 0, tiled=True).sum(0)
    spread = jnp.broadcast_to(mine[None], (devices, per, width))
    total = lax.all_to_all(spread, every, 0, 0, tiled=True).reshape(devices * per, width)
    kernel_sum = total[: KS * KS].reshape(KS, KS, width)
    return kernel_sum, total[KS * KS], total[KS * KS + 1]


def body(feature_maps, dw_kernel, norm_gain, w_up, w_down, layer_scale, d_out):
    scenes, strip, across, width = feature_maps.shape
    cells = scenes * strip * across
    hid_axes = ("fsdp", "rows")
    mine = lax.all_to_all(jnp.stack([w_up, w_down.T]), "rows", 2, 1, tiled=True)
    both = lax.all_gather(mine, "dp", axis=1, tiled=True)
    up_loc, down_t = both[0], both[1]
    cotan = d_out.reshape(cells, width).astype(jnp.float32)
    back = (cotan * layer_scale).astype(jnp.bfloat16)
    rimmed = padded_2(feature_maps, (("rows", 1),), 3)
    padded = jnp.pad(rimmed.astype(jnp.float32), ((0, 0), (0, 0), (3, 3), (0, 0)))
    filtered = jnp.zeros(feature_maps.shape, jnp.float32)
    for row_off in range(KS):
        for col_off in range(KS):
            filtered = (
                filtered
                + padded[:, row_off : row_off + strip, col_off : col_off + across, :]
                * dw_kernel[row_off, col_off]
            )
    flat = filtered.reshape(cells, width)
    average = jnp.mean(flat, axis=-1, keepdims=True)
    center = flat - average
    variance = jnp.mean(center * center, axis=-1, keepdims=True)
    rstd = lax.rsqrt(variance + norm_eps)
    normed = center * rstd
    scaled = (normed * norm_gain).astype(jnp.bfloat16)
    pair = lax.all_gather(jnp.stack([scaled, back]), hid_axes, axis=1, tiled=True)
    gathered, back_all = pair[0], pair[1]
    hidden = jnp.dot(gathered, up_loc, preferred_element_type=jnp.float32)
    active = gelu_exact(hidden).astype(jnp.bfloat16)
    mlp_terms = lax.dot_general(
        active, down_t, contract_cols, preferred_element_type=jnp.float32
    )
    down_part_t = lax.dot_general(
        back_all, active, contract_rows, preferred_element_type=jnp.float32
    )
    slope_in = jnp.dot(back_all, down_t, preferred_element_type=jnp.float32)
    hidden_grad = (slope_in * gelu_slope(hidden)).astype(jnp.bfloat16)
    up_part = lax.dot_general(
        gathered, hidden_grad, contract_rows, preferred_element_type=jnp.float32
    )
    norm_terms = lax.dot_general(
        hidden_grad, up_loc, contract_cols, preferred_element_type=jnp.float32
    )
    sums = lax.psum_scatter(
        jnp.stack([mlp_terms, norm_terms]).astype(jnp.bfloat16),
        hid_axes,
        scatter_dimension=1,
        tiled=True,
    ).astype(jnp.float32)
    branch, norm_grad = sums[0], sums[1]
    resid = feature_maps.reshape(cells, width).astype(jnp.float32)
    result = (resid + layer_scale * branch).astype(jnp.bfloat16).reshape(feature_maps.shape)
    scale_part = jnp.sum(cotan * branch, axis=0)
    grad_parts = jnp.stack([up_part, down_part_t]).astype(jnp.bfloat16)
    grad_sums = lax.psum_scatter(grad_parts, "dp", scatter_dimension=1, tiled=True)
    gain_part = jnp.sum(norm_grad * normed, axis=0)
    scaled_grad = norm_grad * norm_gain
    conv_grad = rstd * (
        scaled_grad
        - jnp.mean(scaled_grad, axis=-1, keepdims=True)
        - normed * jnp.mean(scaled_grad * normed, axis=-1, keepdims=True)
    )
    conv_grad = conv_grad.reshape(feature_maps.shape)
    grad_rim = padded_2(conv_grad.astype(jnp.bfloat16), (("rows", 1),), 3).astype(conv_grad.dtype)
    grad_pad = jnp.pad(grad_rim, ((0, 0), (0, 0), (3, 3), (0, 0)))
    kernel_rows = []
    back_conv = jnp.zeros(feature_maps.shape, jnp.float32)
    for row_off in range(KS):
        for col_off in range(KS):
            window = padded[:, row_off : row_off + strip, col_off : col_off + across, :]
            kernel_rows.append(jnp.sum(window * conv_grad, axis=(0, 1, 2)))
            back_conv = (
                back_conv
                + grad_pad[
                    :, 6 - row_off : 6 - row_off + strip, 6 - col_off : 6 - col_off + across, :
                ]
                * dw_kernel[row_off, col_off]
            )
    kernel_part = jnp.stack(kernel_rows).reshape(KS, KS, width)
    grad_x = (d_out.astype(jnp.float32) + back_conv).astype(jnp.bfloat16)
    grad_kernel, grad_gain, grad_scale = small_sums(kernel_part, gain_part, scale_part, width)
    grad_sums, grad_x, grad_kernel, grad_gain, grad_scale = lax.optimization_barrier(
        (grad_sums, grad_x, grad_kernel, grad_gain, grad_scale)
    )
    grad_up = lax.all_to_all(grad_sums[0], "rows", 0, 1, tiled=True).astype(jnp.float32)
    grad_down = lax.all_to_all(grad_sums[1], "rows", 0, 1, tiled=True).T.astype(jnp.float32)
    return (result, grad_x, grad_up, grad_down, grad_kernel, grad_gain, grad_scale)


def solution(mesh):
    return jax.shard_map(
        body,
        mesh=mesh,
        in_specs=(
            P(("dp", "fsdp"), "rows", None, None),
            P(),
            P(),
            P(("dp", "rows"), "fsdp"),
            P("fsdp", ("dp", "rows")),
            P(),
            P(("dp", "fsdp"), "rows", None, None),
        ),
        out_specs=(
            P(("dp", "fsdp"), "rows", None, None),
            P(("dp", "fsdp"), "rows", None, None),
            P(("dp", "rows"), "fsdp"),
            P("fsdp", ("dp", "rows")),
            P(),
            P(),
            P(),
        ),
        check_vma=False,
    )
```

```python
import math

import jax
import jax.numpy as jnp
from jax import lax
from jax.sharding import PartitionSpec as P

KS = 7


norm_eps = 1e-06
inv_root_two = 1.0 / math.sqrt(2.0)
inv_root_two_pi = 1.0 / math.sqrt(2.0 * math.pi)
contract_rows = (((0,), (0,)), ((), ()))
contract_cols = (((1,), (1,)), ((), ()))


def padded_2(x, sides, width):
    for axis, dim in sides:
        devices, length = (lax.axis_size(axis), x.shape[dim])
        up = [(i, (i + 1) % devices) for i in range(devices - 1)]
        down = [(j, i) for i, j in up]
        last = lax.slice_in_dim(x, length - width, length, axis=dim)
        leading = lax.slice_in_dim(x, 0, width, axis=dim)
        before = lax.ppermute(last, axis, up)
        after = lax.ppermute(leading, axis, down)
        x = jnp.concatenate([before, x, after], axis=dim)
    return x


def gelu_exact(values):
    return 0.5 * values * (1.0 + jax.scipy.special.erf(values * inv_root_two))


def gelu_slope(values):
    cdf_part = 0.5 * (1.0 + jax.scipy.special.erf(values * inv_root_two))
    return cdf_part + values * jnp.exp(-0.5 * values * values) * inv_root_two_pi


def small_sums(kernel_part, gain_part, scale_part, width):
    every = ("dp", "fsdp", "rows")
    devices = lax.axis_size(every)
    packed = jnp.concatenate(
        [kernel_part.reshape(KS * KS, width), gain_part[None], scale_part[None]], axis=0
    )
    count = packed.shape[0]
    per = -(-count // devices)
    packed = jnp.pad(packed, ((0, per * devices - count), (0, 0)))
    mine = lax.all_to_all(packed.reshape(devices, per, width), every, 0, 0, tiled=True).sum(0)
    spread = jnp.broadcast_to(mine[None], (devices, per, width))
    total = lax.all_to_all(spread, every, 0, 0, tiled=True).reshape(devices * per, width)
    kernel_sum = total[: KS * KS].reshape(KS, KS, width)
    return kernel_sum, total[KS * KS], total[KS * KS + 1]


def body(feature_maps, dw_kernel, norm_gain, w_up, w_down, layer_scale, d_out):
    scenes, strip, across, width = feature_maps.shape
    cells = scenes * strip * across
    hid_axes = ("fsdp", "rows")
    dp_size, row_size = lax.axis_size("dp"), lax.axis_size("rows")
    block_c, hid_f = w_up.shape
    sub = hid_f // row_size
    pieces = jnp.stack([w_up, w_down.T]).reshape(2, block_c, row_size, sub).transpose(0, 2, 1, 3)
    pieces = jnp.broadcast_to(pieces[:, None], (2, dp_size, row_size, block_c, sub))
    pieces = pieces.reshape(2, dp_size * row_size, block_c, sub)
    both = lax.all_to_all(pieces, ("dp", "rows"), 1, 1, tiled=True)
    both = both.reshape(2, dp_size * row_size * block_c, sub)
    up_loc, down_t = both[0], both[1]
    cotan = d_out.reshape(cells, width).astype(jnp.float32)
    back = (cotan * layer_scale).astype(jnp.bfloat16)
    rimmed = padded_2(feature_maps, (("rows", 1),), 3)
    padded = jnp.pad(rimmed.astype(jnp.float32), ((0, 0), (0, 0), (3, 3), (0, 0)))
    filtered = jnp.zeros(feature_maps.shape, jnp.float32)
    for row_off in range(KS):
        for col_off in range(KS):
            filtered = (
                filtered
                + padded[:, row_off : row_off + strip, col_off : col_off + across, :]
                * dw_kernel[row_off, col_off]
            )
    flat = filtered.reshape(cells, width)
    average = jnp.mean(flat, axis=-1, keepdims=True)
    center = flat - average
    variance = jnp.mean(center * center, axis=-1, keepdims=True)
    rstd = lax.rsqrt(variance + norm_eps)
    normed = center * rstd
    scaled = (normed * norm_gain).astype(jnp.bfloat16)
    pair = lax.all_gather(jnp.stack([scaled, back]), hid_axes, axis=1, tiled=True)
    gathered, back_all = pair[0], pair[1]
    hidden = jnp.dot(gathered, up_loc, preferred_element_type=jnp.float32)
    active = gelu_exact(hidden).astype(jnp.bfloat16)
    mlp_terms = lax.dot_general(
        active, down_t, contract_cols, preferred_element_type=jnp.float32
    )
    down_part_t = lax.dot_general(
        back_all, active, contract_rows, preferred_element_type=jnp.float32
    )
    slope_in = jnp.dot(back_all, down_t, preferred_element_type=jnp.float32)
    hidden_grad = (slope_in * gelu_slope(hidden)).astype(jnp.bfloat16)
    up_part = lax.dot_general(
        gathered, hidden_grad, contract_rows, preferred_element_type=jnp.float32
    )
    norm_terms = lax.dot_general(
        hidden_grad, up_loc, contract_cols, preferred_element_type=jnp.float32
    )
    sums = lax.psum_scatter(
        jnp.stack([mlp_terms, norm_terms]).astype(jnp.bfloat16),
        hid_axes,
        scatter_dimension=1,
        tiled=True,
    ).astype(jnp.float32)
    branch, norm_grad = sums[0], sums[1]
    resid = feature_maps.reshape(cells, width).astype(jnp.float32)
    result = (resid + layer_scale * branch).astype(jnp.bfloat16).reshape(feature_maps.shape)
    scale_part = jnp.sum(cotan * branch, axis=0)
    grad_parts = jnp.stack([up_part, down_part_t]).astype(jnp.bfloat16)
    grad_sums = lax.psum_scatter(grad_parts, "dp", scatter_dimension=1, tiled=True)
    gain_part = jnp.sum(norm_grad * normed, axis=0)
    scaled_grad = norm_grad * norm_gain
    conv_grad = rstd * (
        scaled_grad
        - jnp.mean(scaled_grad, axis=-1, keepdims=True)
        - normed * jnp.mean(scaled_grad * normed, axis=-1, keepdims=True)
    )
    conv_grad = conv_grad.reshape(feature_maps.shape)
    grad_rim = padded_2(conv_grad.astype(jnp.bfloat16), (("rows", 1),), 3).astype(conv_grad.dtype)
    grad_pad = jnp.pad(grad_rim, ((0, 0), (0, 0), (3, 3), (0, 0)))
    kernel_rows = []
    back_conv = jnp.zeros(feature_maps.shape, jnp.float32)
    for row_off in range(KS):
        for col_off in range(KS):
            window = padded[:, row_off : row_off + strip, col_off : col_off + across, :]
            kernel_rows.append(jnp.sum(window * conv_grad, axis=(0, 1, 2)))
            back_conv = (
                back_conv
                + grad_pad[
                    :, 6 - row_off : 6 - row_off + strip, 6 - col_off : 6 - col_off + across, :
                ]
                * dw_kernel[row_off, col_off]
            )
    kernel_part = jnp.stack(kernel_rows).reshape(KS, KS, width)
    grad_x = (d_out.astype(jnp.float32) + back_conv).astype(jnp.bfloat16)
    grad_kernel, grad_gain, grad_scale = small_sums(kernel_part, gain_part, scale_part, width)
    grad_sums, grad_x, grad_kernel, grad_gain, grad_scale = lax.optimization_barrier(
        (grad_sums, grad_x, grad_kernel, grad_gain, grad_scale)
    )
    grad_sums = lax.all_to_all(grad_sums, "rows", 1, 2, tiled=True).astype(jnp.float32)
    grad_up, grad_down = grad_sums[0], grad_sums[1].T
    return (result, grad_x, grad_up, grad_down, grad_kernel, grad_gain, grad_scale)


def solution(mesh):
    return jax.shard_map(
        body,
        mesh=mesh,
        in_specs=(
            P(("dp", "fsdp"), "rows", None, None),
            P(),
            P(),
            P(("dp", "rows"), "fsdp"),
            P("fsdp", ("dp", "rows")),
            P(),
            P(("dp", "fsdp"), "rows", None, None),
        ),
        out_specs=(
            P(("dp", "fsdp"), "rows", None, None),
            P(("dp", "fsdp"), "rows", None, None),
            P(("dp", "rows"), "fsdp"),
            P("fsdp", ("dp", "rows")),
            P(),
            P(),
            P(),
        ),
        check_vma=False,
    )
```

```python
import math

import jax
import jax.numpy as jnp
from jax import lax
from jax.sharding import PartitionSpec as P

KS = 7


norm_eps = 1e-06
inv_root_two = 1.0 / math.sqrt(2.0)
inv_root_two_pi = 1.0 / math.sqrt(2.0 * math.pi)
contract_rows = (((0,), (0,)), ((), ()))
contract_cols = (((1,), (1,)), ((), ()))


def padded_2(x, sides, width):
    for axis, dim in sides:
        devices, length = (lax.axis_size(axis), x.shape[dim])
        up = [(i, (i + 1) % devices) for i in range(devices - 1)]
        down = [(j, i) for i, j in up]
        last = lax.slice_in_dim(x, length - width, length, axis=dim)
        leading = lax.slice_in_dim(x, 0, width, axis=dim)
        before = lax.ppermute(last, axis, up)
        after = lax.ppermute(leading, axis, down)
        x = jnp.concatenate([before, x, after], axis=dim)
    return x


def gelu_exact(values):
    return 0.5 * values * (1.0 + jax.scipy.special.erf(values * inv_root_two))


def gelu_slope(values):
    cdf_part = 0.5 * (1.0 + jax.scipy.special.erf(values * inv_root_two))
    return cdf_part + values * jnp.exp(-0.5 * values * values) * inv_root_two_pi


def small_sums(kernel_part, gain_part, scale_part, width):
    every = ("dp", "fsdp", "rows")
    devices = lax.axis_size(every)
    packed = jnp.concatenate(
        [kernel_part.reshape(KS * KS, width), gain_part[None], scale_part[None]], axis=0
    )
    count = packed.shape[0]
    per = -(-count // devices)
    packed = jnp.pad(packed, ((0, per * devices - count), (0, 0)))
    mine = lax.all_to_all(packed.reshape(devices, per, width), every, 0, 0, tiled=True).sum(0)
    spread = jnp.broadcast_to(mine[None], (devices, per, width))
    total = lax.all_to_all(spread, every, 0, 0, tiled=True).reshape(devices * per, width)
    kernel_sum = total[: KS * KS].reshape(KS, KS, width)
    return kernel_sum, total[KS * KS], total[KS * KS + 1]


def body(feature_maps, dw_kernel, norm_gain, w_up, w_down, layer_scale, d_out):
    scenes, strip, across, width = feature_maps.shape
    cells = scenes * strip * across
    hid_axes = ("fsdp", "rows")
    dp_size, row_size = lax.axis_size("dp"), lax.axis_size("rows")
    block_c, hid_f = w_up.shape
    sub = hid_f // row_size
    pieces = jnp.stack([w_up, w_down.T]).reshape(2, block_c, row_size, sub).transpose(0, 2, 1, 3)
    pieces = jnp.broadcast_to(pieces[:, None], (2, dp_size, row_size, block_c, sub))
    pieces = pieces.reshape(2, dp_size * row_size, block_c, sub)
    both = lax.all_to_all(pieces, ("dp", "rows"), 1, 1, tiled=True)
    both = both.reshape(2, dp_size * row_size * block_c, sub)
    up_loc, down_t = both[0], both[1]
    cotan = d_out.reshape(cells, width).astype(jnp.float32)
    back = (cotan * layer_scale).astype(jnp.bfloat16)
    rimmed = padded_2(feature_maps, (("rows", 1),), 3)
    padded = jnp.pad(rimmed.astype(jnp.float32), ((0, 0), (0, 0), (3, 3), (0, 0)))
    filtered = jnp.zeros(feature_maps.shape, jnp.float32)
    for row_off in range(KS):
        for col_off in range(KS):
            filtered = (
                filtered
                + padded[:, row_off : row_off + strip, col_off : col_off + across, :]
                * dw_kernel[row_off, col_off]
            )
    flat = filtered.reshape(cells, width)
    average = jnp.mean(flat, axis=-1, keepdims=True)
    center = flat - average
    variance = jnp.mean(center * center, axis=-1, keepdims=True)
    rstd = lax.rsqrt(variance + norm_eps)
    normed = center * rstd
    scaled = (normed * norm_gain).astype(jnp.bfloat16)
    pair = lax.all_gather(jnp.stack([scaled, back]), hid_axes, axis=1, tiled=True)
    gathered, back_all = pair[0], pair[1]
    hidden = jnp.dot(gathered, up_loc, preferred_element_type=jnp.float32)
    active = gelu_exact(hidden).astype(jnp.bfloat16)
    mlp_terms = lax.dot_general(
        active, down_t, contract_cols, preferred_element_type=jnp.float32
    )
    slope_in = jnp.dot(back_all, down_t, preferred_element_type=jnp.float32)
    hidden_grad = (slope_in * gelu_slope(hidden)).astype(jnp.bfloat16)
    norm_terms = lax.dot_general(
        hidden_grad, up_loc, contract_cols, preferred_element_type=jnp.float32
    )
    to_sum = jnp.stack([mlp_terms, norm_terms]).astype(jnp.bfloat16)
    to_sum, gathered, back_all, active, hidden_grad = lax.optimization_barrier(
        (to_sum, gathered, back_all, active, hidden_grad)
    )
    sums = lax.psum_scatter(to_sum, hid_axes, scatter_dimension=1, tiled=True).astype(
        jnp.float32
    )
    down_part_t = lax.dot_general(
        back_all, active, contract_rows, preferred_element_type=jnp.float32
    )
    up_part = lax.dot_general(
        gathered, hidden_grad, contract_rows, preferred_element_type=jnp.float32
    )
    branch, norm_grad = sums[0], sums[1]
    resid = feature_maps.reshape(cells, width).astype(jnp.float32)
    result = (resid + layer_scale * branch).astype(jnp.bfloat16).reshape(feature_maps.shape)
    scale_part = jnp.sum(cotan * branch, axis=0)
    grad_parts = jnp.stack([up_part, down_part_t]).astype(jnp.bfloat16)
    grad_sums = lax.psum_scatter(grad_parts, "dp", scatter_dimension=1, tiled=True)
    gain_part = jnp.sum(norm_grad * normed, axis=0)
    scaled_grad = norm_grad * norm_gain
    conv_grad = rstd * (
        scaled_grad
        - jnp.mean(scaled_grad, axis=-1, keepdims=True)
        - normed * jnp.mean(scaled_grad * normed, axis=-1, keepdims=True)
    )
    conv_grad = conv_grad.reshape(feature_maps.shape)
    grad_rim = padded_2(conv_grad.astype(jnp.bfloat16), (("rows", 1),), 3).astype(conv_grad.dtype)
    grad_pad = jnp.pad(grad_rim, ((0, 0), (0, 0), (3, 3), (0, 0)))
    kernel_rows = []
    back_conv = jnp.zeros(feature_maps.shape, jnp.float32)
    for row_off in range(KS):
        for col_off in range(KS):
            window = padded[:, row_off : row_off + strip, col_off : col_off + across, :]
            kernel_rows.append(jnp.sum(window * conv_grad, axis=(0, 1, 2)))
            back_conv = (
                back_conv
                + grad_pad[
                    :, 6 - row_off : 6 - row_off + strip, 6 - col_off : 6 - col_off + across, :
                ]
                * dw_kernel[row_off, col_off]
            )
    kernel_part = jnp.stack(kernel_rows).reshape(KS, KS, width)
    grad_x = (d_out.astype(jnp.float32) + back_conv).astype(jnp.bfloat16)
    grad_kernel, grad_gain, grad_scale = small_sums(kernel_part, gain_part, scale_part, width)
    grad_sums, grad_x, grad_kernel, grad_gain, grad_scale = lax.optimization_barrier(
        (grad_sums, grad_x, grad_kernel, grad_gain, grad_scale)
    )
    grad_sums = lax.all_to_all(grad_sums, "rows", 1, 2, tiled=True).astype(jnp.float32)
    grad_up, grad_down = grad_sums[0], grad_sums[1].T
    return (result, grad_x, grad_up, grad_down, grad_kernel, grad_gain, grad_scale)


def solution(mesh):
    return jax.shard_map(
        body,
        mesh=mesh,
        in_specs=(
            P(("dp", "fsdp"), "rows", None, None),
            P(),
            P(),
            P(("dp", "rows"), "fsdp"),
            P("fsdp", ("dp", "rows")),
            P(),
            P(("dp", "fsdp"), "rows", None, None),
        ),
        out_specs=(
            P(("dp", "fsdp"), "rows", None, None),
            P(("dp", "fsdp"), "rows", None, None),
            P(("dp", "rows"), "fsdp"),
            P("fsdp", ("dp", "rows")),
            P(),
            P(),
            P(),
        ),
        check_vma=False,
    )
```

```python
import math

import jax
import jax.numpy as jnp
from jax import lax
from jax.sharding import PartitionSpec as P

KS = 7


norm_eps = 1e-06
inv_root_two = 1.0 / math.sqrt(2.0)
inv_root_two_pi = 1.0 / math.sqrt(2.0 * math.pi)
contract_rows = (((0,), (0,)), ((), ()))
contract_cols = (((1,), (1,)), ((), ()))


def padded_2(x, sides, width):
    for axis, dim in sides:
        devices, length = (lax.axis_size(axis), x.shape[dim])
        up = [(i, (i + 1) % devices) for i in range(devices - 1)]
        down = [(j, i) for i, j in up]
        last = lax.slice_in_dim(x, length - width, length, axis=dim)
        leading = lax.slice_in_dim(x, 0, width, axis=dim)
        before = lax.ppermute(last, axis, up)
        after = lax.ppermute(leading, axis, down)
        x = jnp.concatenate([before, x, after], axis=dim)
    return x


def gelu_exact(values):
    return 0.5 * values * (1.0 + jax.scipy.special.erf(values * inv_root_two))


def gelu_slope(values):
    cdf_part = 0.5 * (1.0 + jax.scipy.special.erf(values * inv_root_two))
    return cdf_part + values * jnp.exp(-0.5 * values * values) * inv_root_two_pi


def small_sums(kernel_part, gain_part, scale_part, width):
    every = ("dp", "fsdp", "rows")
    devices = lax.axis_size(every)
    packed = jnp.concatenate(
        [kernel_part.reshape(KS * KS, width), gain_part[None], scale_part[None]], axis=0
    )
    count = packed.shape[0]
    per = -(-count // devices)
    packed = jnp.pad(packed, ((0, per * devices - count), (0, 0)))
    mine = lax.all_to_all(packed.reshape(devices, per, width), every, 0, 0, tiled=True).sum(0)
    spread = jnp.broadcast_to(mine[None], (devices, per, width))
    total = lax.all_to_all(spread, every, 0, 0, tiled=True).reshape(devices * per, width)
    kernel_sum = total[: KS * KS].reshape(KS, KS, width)
    return kernel_sum, total[KS * KS], total[KS * KS + 1]


def body(feature_maps, dw_kernel, norm_gain, w_up, w_down, layer_scale, d_out):
    scenes, strip, across, width = feature_maps.shape
    cells = scenes * strip * across
    hid_axes = ("fsdp", "rows")
    dp_size, row_size = lax.axis_size("dp"), lax.axis_size("rows")
    block_c, hid_f = w_up.shape
    sub = hid_f // row_size
    pieces = jnp.stack([w_up, w_down.T]).reshape(2, block_c, row_size, sub).transpose(0, 2, 1, 3)
    pieces = jnp.broadcast_to(pieces[:, None], (2, dp_size, row_size, block_c, sub))
    pieces = pieces.reshape(2, dp_size * row_size, block_c, sub)
    both = lax.all_to_all(pieces, ("dp", "rows"), 1, 1, tiled=True)
    both = both.reshape(2, dp_size * row_size * block_c, sub)
    up_loc, down_t = both[0], both[1]
    cotan = d_out.reshape(cells, width).astype(jnp.float32)
    back = (cotan * layer_scale).astype(jnp.bfloat16)
    rimmed = padded_2(feature_maps, (("rows", 1),), 3)
    padded = jnp.pad(rimmed.astype(jnp.float32), ((0, 0), (0, 0), (3, 3), (0, 0)))
    filtered = jnp.zeros(feature_maps.shape, jnp.float32)
    for row_off in range(KS):
        for col_off in range(KS):
            filtered = (
                filtered
                + padded[:, row_off : row_off + strip, col_off : col_off + across, :]
                * dw_kernel[row_off, col_off]
            )
    flat = filtered.reshape(cells, width)
    average = jnp.mean(flat, axis=-1, keepdims=True)
    center = flat - average
    variance = jnp.mean(center * center, axis=-1, keepdims=True)
    rstd = lax.rsqrt(variance + norm_eps)
    normed = center * rstd
    scaled = (normed * norm_gain).astype(jnp.bfloat16)
    pair = lax.all_gather(jnp.stack([scaled, back]), hid_axes, axis=1, tiled=True)
    gathered, back_all = pair[0], pair[1]
    hidden = jnp.dot(gathered, up_loc, preferred_element_type=jnp.float32)
    active = gelu_exact(hidden).astype(jnp.bfloat16)
    mlp_terms = lax.dot_general(
        active, down_t, contract_cols, preferred_element_type=jnp.float32
    )
    down_part_t = lax.dot_general(
        back_all, active, contract_rows, preferred_element_type=jnp.float32
    )
    slope_in = jnp.dot(back_all, down_t, preferred_element_type=jnp.float32)
    hidden_grad = (slope_in * gelu_slope(hidden)).astype(jnp.bfloat16)
    up_part = lax.dot_general(
        gathered, hidden_grad, contract_rows, preferred_element_type=jnp.float32
    )
    norm_terms = lax.dot_general(
        hidden_grad, up_loc, contract_cols, preferred_element_type=jnp.float32
    )
    sums = lax.psum_scatter(
        jnp.stack([mlp_terms, norm_terms]).astype(jnp.bfloat16),
        hid_axes,
        scatter_dimension=1,
        tiled=True,
    ).astype(jnp.float32)
    branch, norm_grad = sums[0], sums[1]
    resid = feature_maps.reshape(cells, width).astype(jnp.float32)
    result = (resid + layer_scale * branch).astype(jnp.bfloat16).reshape(feature_maps.shape)
    scale_part = jnp.sum(cotan * branch, axis=0)
    grad_parts = jnp.stack([up_part, down_part_t]).astype(jnp.bfloat16)
    grad_sums = lax.psum_scatter(grad_parts, "dp", scatter_dimension=1, tiled=True)
    gain_part = jnp.sum(norm_grad * normed, axis=0)
    scaled_grad = norm_grad * norm_gain
    conv_grad = rstd * (
        scaled_grad
        - jnp.mean(scaled_grad, axis=-1, keepdims=True)
        - normed * jnp.mean(scaled_grad * normed, axis=-1, keepdims=True)
    )
    conv_grad = conv_grad.reshape(feature_maps.shape)
    grad_rim = padded_2(conv_grad.astype(jnp.bfloat16), (("rows", 1),), 3).astype(conv_grad.dtype)
    grad_pad = jnp.pad(grad_rim, ((0, 0), (0, 0), (3, 3), (0, 0)))
    kernel_rows = []
    back_conv = jnp.zeros(feature_maps.shape, jnp.float32)
    for row_off in range(KS):
        for col_off in range(KS):
            window = padded[:, row_off : row_off + strip, col_off : col_off + across, :]
            kernel_rows.append(jnp.sum(window * conv_grad, axis=(0, 1, 2)))
            back_conv = (
                back_conv
                + grad_pad[
                    :, 6 - row_off : 6 - row_off + strip, 6 - col_off : 6 - col_off + across, :
                ]
                * dw_kernel[row_off, col_off]
            )
    kernel_part = jnp.stack(kernel_rows).reshape(KS, KS, width)
    grad_x = (d_out.astype(jnp.float32) + back_conv).astype(jnp.bfloat16)
    grad_sums, grad_x, kernel_part, gain_part, scale_part = lax.optimization_barrier(
        (grad_sums, grad_x, kernel_part, gain_part, scale_part)
    )
    grad_kernel, grad_gain, grad_scale = small_sums(kernel_part, gain_part, scale_part, width)
    grad_sums = lax.all_to_all(grad_sums, "rows", 1, 2, tiled=True).astype(jnp.float32)
    grad_up, grad_down = grad_sums[0], grad_sums[1].T
    return (result, grad_x, grad_up, grad_down, grad_kernel, grad_gain, grad_scale)


def solution(mesh):
    return jax.shard_map(
        body,
        mesh=mesh,
        in_specs=(
            P(("dp", "fsdp"), "rows", None, None),
            P(),
            P(),
            P(("dp", "rows"), "fsdp"),
            P("fsdp", ("dp", "rows")),
            P(),
            P(("dp", "fsdp"), "rows", None, None),
        ),
        out_specs=(
            P(("dp", "fsdp"), "rows", None, None),
            P(("dp", "fsdp"), "rows", None, None),
            P(("dp", "rows"), "fsdp"),
            P("fsdp", ("dp", "rows")),
            P(),
            P(),
            P(),
        ),
        check_vma=False,
    )
```

```python
import math

import jax
import jax.numpy as jnp
from jax import lax
from jax.sharding import PartitionSpec as P

KS = 7


norm_eps = 1e-06
inv_root_two = 1.0 / math.sqrt(2.0)
inv_root_two_pi = 1.0 / math.sqrt(2.0 * math.pi)
contract_rows = (((0,), (0,)), ((), ()))
contract_cols = (((1,), (1,)), ((), ()))


def padded_2(x, sides, width):
    for axis, dim in sides:
        devices, length = (lax.axis_size(axis), x.shape[dim])
        up = [(i, (i + 1) % devices) for i in range(devices - 1)]
        down = [(j, i) for i, j in up]
        last = lax.slice_in_dim(x, length - width, length, axis=dim)
        leading = lax.slice_in_dim(x, 0, width, axis=dim)
        before = lax.ppermute(last, axis, up)
        after = lax.ppermute(leading, axis, down)
        x = jnp.concatenate([before, x, after], axis=dim)
    return x


def gelu_exact(values):
    return 0.5 * values * (1.0 + jax.scipy.special.erf(values * inv_root_two))


def gelu_slope(values):
    cdf_part = 0.5 * (1.0 + jax.scipy.special.erf(values * inv_root_two))
    return cdf_part + values * jnp.exp(-0.5 * values * values) * inv_root_two_pi


def small_sums(kernel_part, gain_part, scale_part, width):
    every = ("dp", "fsdp", "rows")
    devices = lax.axis_size(every)
    packed = jnp.concatenate(
        [kernel_part.reshape(KS * KS, width), gain_part[None], scale_part[None]], axis=0
    )
    count = packed.shape[0]
    per = -(-count // devices)
    packed = jnp.pad(packed, ((0, per * devices - count), (0, 0)))
    mine = lax.all_to_all(packed.reshape(devices, per, width), every, 0, 0, tiled=True).sum(0)
    spread = jnp.broadcast_to(mine[None], (devices, per, width))
    total = lax.all_to_all(spread, every, 0, 0, tiled=True).reshape(devices * per, width)
    kernel_sum = total[: KS * KS].reshape(KS, KS, width)
    return kernel_sum, total[KS * KS], total[KS * KS + 1]


def body(feature_maps, dw_kernel, norm_gain, w_up, w_down, layer_scale, d_out):
    scenes, strip, across, width = feature_maps.shape
    cells = scenes * strip * across
    hid_axes = ("fsdp", "rows")
    dp_size, row_size = lax.axis_size("dp"), lax.axis_size("rows")
    block_c, hid_f = w_up.shape
    sub = hid_f // row_size
    pieces = w_up.reshape(block_c, row_size, sub).transpose(1, 0, 2)
    pieces = jnp.broadcast_to(pieces[None], (dp_size, row_size, block_c, sub))
    pieces = pieces.reshape(dp_size * row_size, block_c, sub)
    up_loc = lax.all_to_all(pieces, ("dp", "rows"), 0, 0, tiled=True)
    up_loc = up_loc.reshape(dp_size * row_size * block_c, sub)
    down_loc = lax.all_to_all(w_down, "rows", 0, 1, tiled=True)
    down_loc = lax.all_gather(down_loc, "dp", axis=1, tiled=True)
    cotan = d_out.reshape(cells, width).astype(jnp.float32)
    back = (cotan * layer_scale).astype(jnp.bfloat16)
    rimmed = padded_2(feature_maps, (("rows", 1),), 3)
    padded = jnp.pad(rimmed.astype(jnp.float32), ((0, 0), (0, 0), (3, 3), (0, 0)))
    filtered = jnp.zeros(feature_maps.shape, jnp.float32)
    for row_off in range(KS):
        for col_off in range(KS):
            filtered = (
                filtered
                + padded[:, row_off : row_off + strip, col_off : col_off + across, :]
                * dw_kernel[row_off, col_off]
            )
    flat = filtered.reshape(cells, width)
    average = jnp.mean(flat, axis=-1, keepdims=True)
    center = flat - average
    variance = jnp.mean(center * center, axis=-1, keepdims=True)
    rstd = lax.rsqrt(variance + norm_eps)
    normed = center * rstd
    scaled = (normed * norm_gain).astype(jnp.bfloat16)
    pair = lax.all_gather(jnp.stack([scaled, back]), hid_axes, axis=1, tiled=True)
    gathered, back_all = pair[0], pair[1]
    hidden = jnp.dot(gathered, up_loc, preferred_element_type=jnp.float32)
    active = gelu_exact(hidden).astype(jnp.bfloat16)
    mlp_terms = jnp.dot(active, down_loc, preferred_element_type=jnp.float32)
    down_part_t = lax.dot_general(
        back_all, active, contract_rows, preferred_element_type=jnp.float32
    )
    slope_in = lax.dot_general(
        back_all, down_loc, contract_cols, preferred_element_type=jnp.float32
    )
    hidden_grad = (slope_in * gelu_slope(hidden)).astype(jnp.bfloat16)
    up_part = lax.dot_general(
        gathered, hidden_grad, contract_rows, preferred_element_type=jnp.float32
    )
    norm_terms = lax.dot_general(
        hidden_grad, up_loc, contract_cols, preferred_element_type=jnp.float32
    )
    sums = lax.psum_scatter(
        jnp.stack([mlp_terms, norm_terms]).astype(jnp.bfloat16),
        hid_axes,
        scatter_dimension=1,
        tiled=True,
    ).astype(jnp.float32)
    branch, norm_grad = sums[0], sums[1]
    resid = feature_maps.reshape(cells, width).astype(jnp.float32)
    result = (resid + layer_scale * branch).astype(jnp.bfloat16).reshape(feature_maps.shape)
    scale_part = jnp.sum(cotan * branch, axis=0)
    grad_parts = jnp.stack([up_part, down_part_t]).astype(jnp.bfloat16)
    grad_sums = lax.psum_scatter(grad_parts, "dp", scatter_dimension=1, tiled=True)
    gain_part = jnp.sum(norm_grad * normed, axis=0)
    scaled_grad = norm_grad * norm_gain
    conv_grad = rstd * (
        scaled_grad
        - jnp.mean(scaled_grad, axis=-1, keepdims=True)
        - normed * jnp.mean(scaled_grad * normed, axis=-1, keepdims=True)
    )
    conv_grad = conv_grad.reshape(feature_maps.shape)
    grad_rim = padded_2(conv_grad.astype(jnp.bfloat16), (("rows", 1),), 3).astype(conv_grad.dtype)
    grad_pad = jnp.pad(grad_rim, ((0, 0), (0, 0), (3, 3), (0, 0)))
    kernel_rows = []
    back_conv = jnp.zeros(feature_maps.shape, jnp.float32)
    for row_off in range(KS):
        for col_off in range(KS):
            window = padded[:, row_off : row_off + strip, col_off : col_off + across, :]
            kernel_rows.append(jnp.sum(window * conv_grad, axis=(0, 1, 2)))
            back_conv = (
                back_conv
                + grad_pad[
                    :, 6 - row_off : 6 - row_off + strip, 6 - col_off : 6 - col_off + across, :
                ]
                * dw_kernel[row_off, col_off]
            )
    kernel_part = jnp.stack(kernel_rows).reshape(KS, KS, width)
    grad_x = (d_out.astype(jnp.float32) + back_conv).astype(jnp.bfloat16)
    grad_kernel, grad_gain, grad_scale = small_sums(kernel_part, gain_part, scale_part, width)
    grad_sums, grad_x, grad_kernel, grad_gain, grad_scale = lax.optimization_barrier(
        (grad_sums, grad_x, grad_kernel, grad_gain, grad_scale)
    )
    grad_sums = lax.all_to_all(grad_sums, "rows", 1, 2, tiled=True).astype(jnp.float32)
    grad_up, grad_down = grad_sums[0], grad_sums[1].T
    return (result, grad_x, grad_up, grad_down, grad_kernel, grad_gain, grad_scale)


def solution(mesh):
    return jax.shard_map(
        body,
        mesh=mesh,
        in_specs=(
            P(("dp", "fsdp"), "rows", None, None),
            P(),
            P(),
            P(("dp", "rows"), "fsdp"),
            P("fsdp", ("dp", "rows")),
            P(),
            P(("dp", "fsdp"), "rows", None, None),
        ),
        out_specs=(
            P(("dp", "fsdp"), "rows", None, None),
            P(("dp", "fsdp"), "rows", None, None),
            P(("dp", "rows"), "fsdp"),
            P("fsdp", ("dp", "rows")),
            P(),
            P(),
            P(),
        ),
        check_vma=False,
    )
```

```python
import math

import jax
import jax.numpy as jnp
from jax import lax
from jax.sharding import PartitionSpec as P

KS = 7


norm_eps = 1e-06
inv_root_two = 1.0 / math.sqrt(2.0)
inv_root_two_pi = 1.0 / math.sqrt(2.0 * math.pi)
contract_rows = (((0,), (0,)), ((), ()))
contract_cols = (((1,), (1,)), ((), ()))


def padded_2(x, sides, width):
    for axis, dim in sides:
        devices, length = (lax.axis_size(axis), x.shape[dim])
        up = [(i, (i + 1) % devices) for i in range(devices - 1)]
        down = [(j, i) for i, j in up]
        last = lax.slice_in_dim(x, length - width, length, axis=dim)
        leading = lax.slice_in_dim(x, 0, width, axis=dim)
        before = lax.ppermute(last, axis, up)
        after = lax.ppermute(leading, axis, down)
        x = jnp.concatenate([before, x, after], axis=dim)
    return x


def gelu_exact(values):
    return 0.5 * values * (1.0 + jax.scipy.special.erf(values * inv_root_two))


def gelu_slope(values):
    cdf_part = 0.5 * (1.0 + jax.scipy.special.erf(values * inv_root_two))
    return cdf_part + values * jnp.exp(-0.5 * values * values) * inv_root_two_pi


def small_sums(kernel_part, gain_part, scale_part, width):
    every = ("dp", "fsdp", "rows")
    devices = lax.axis_size(every)
    packed = jnp.concatenate(
        [kernel_part.reshape(KS * KS, width), gain_part[None], scale_part[None]], axis=0
    )
    count = packed.shape[0]
    per = -(-count // devices)
    packed = jnp.pad(packed, ((0, per * devices - count), (0, 0)))
    mine = lax.all_to_all(packed.reshape(devices, per, width), every, 0, 0, tiled=True).sum(0)
    spread = jnp.broadcast_to(mine[None], (devices, per, width))
    total = lax.all_to_all(spread, every, 0, 0, tiled=True).reshape(devices * per, width)
    kernel_sum = total[: KS * KS].reshape(KS, KS, width)
    return kernel_sum, total[KS * KS], total[KS * KS + 1]


def body(feature_maps, dw_kernel, norm_gain, w_up, w_down, layer_scale, d_out):
    scenes, strip, across, width = feature_maps.shape
    cells = scenes * strip * across
    hid_axes = ("fsdp", "rows")
    dp_size, row_size = lax.axis_size("dp"), lax.axis_size("rows")
    block_c, hid_f = w_up.shape
    sub = hid_f // row_size
    pieces = w_up.reshape(block_c, row_size, sub).transpose(1, 0, 2)
    pieces = jnp.broadcast_to(pieces[None], (dp_size, row_size, block_c, sub))
    pieces = pieces.reshape(dp_size * row_size, block_c, sub)
    up_loc = lax.all_to_all(pieces, ("dp", "rows"), 0, 0, tiled=True)
    up_loc = up_loc.reshape(dp_size * row_size * block_c, sub)
    down_loc = lax.all_to_all(w_down, "rows", 0, 1, tiled=True)
    down_loc = lax.all_gather(down_loc, "dp", axis=1, tiled=True)
    cotan = d_out.reshape(cells, width).astype(jnp.float32)
    back = (cotan * layer_scale).astype(jnp.bfloat16)
    rimmed = padded_2(feature_maps, (("rows", 1),), 3)
    padded = jnp.pad(rimmed.astype(jnp.float32), ((0, 0), (0, 0), (3, 3), (0, 0)))
    filtered = jnp.zeros(feature_maps.shape, jnp.float32)
    for row_off in range(KS):
        for col_off in range(KS):
            filtered = (
                filtered
                + padded[:, row_off : row_off + strip, col_off : col_off + across, :]
                * dw_kernel[row_off, col_off]
            )
    flat = filtered.reshape(cells, width)
    average = jnp.mean(flat, axis=-1, keepdims=True)
    center = flat - average
    variance = jnp.mean(center * center, axis=-1, keepdims=True)
    rstd = lax.rsqrt(variance + norm_eps)
    normed = center * rstd
    scaled = (normed * norm_gain).astype(jnp.bfloat16)
    pair = lax.all_gather(jnp.stack([scaled, back]), hid_axes, axis=1, tiled=True)
    gathered, back_all = pair[0], pair[1]
    hidden = jnp.dot(gathered, up_loc, preferred_element_type=jnp.float32)
    active = gelu_exact(hidden).astype(jnp.bfloat16)
    mlp_terms = jnp.dot(active, down_loc, preferred_element_type=jnp.float32)
    down_part_t = lax.dot_general(
        back_all, active, contract_rows, preferred_element_type=jnp.float32
    )
    slope_in = lax.dot_general(
        back_all, down_loc, contract_cols, preferred_element_type=jnp.float32
    )
    hidden_grad = (slope_in * gelu_slope(hidden)).astype(jnp.bfloat16)
    up_part = lax.dot_general(
        gathered, hidden_grad, contract_rows, preferred_element_type=jnp.float32
    )
    norm_terms = lax.dot_general(
        hidden_grad, up_loc, contract_cols, preferred_element_type=jnp.float32
    )
    sums = lax.psum_scatter(
        jnp.stack([mlp_terms, norm_terms]).astype(jnp.bfloat16),
        hid_axes,
        scatter_dimension=1,
        tiled=True,
    ).astype(jnp.float32)
    branch, norm_grad = sums[0], sums[1]
    resid = feature_maps.reshape(cells, width).astype(jnp.float32)
    result = (resid + layer_scale * branch).astype(jnp.bfloat16).reshape(feature_maps.shape)
    scale_part = jnp.sum(cotan * branch, axis=0)
    down_blocks = down_part_t.astype(jnp.bfloat16).reshape(dp_size, -1, sub)
    down_sum = lax.all_to_all(down_blocks, "dp", 0, 0, tiled=True).astype(jnp.float32).sum(0)
    up_sum = lax.psum_scatter(
        up_part.astype(jnp.bfloat16), "dp", scatter_dimension=0, tiled=True
    ).astype(jnp.float32)
    grad_sums = jnp.stack([up_sum, down_sum])
    gain_part = jnp.sum(norm_grad * normed, axis=0)
    scaled_grad = norm_grad * norm_gain
    conv_grad = rstd * (
        scaled_grad
        - jnp.mean(scaled_grad, axis=-1, keepdims=True)
        - normed * jnp.mean(scaled_grad * normed, axis=-1, keepdims=True)
    )
    conv_grad = conv_grad.reshape(feature_maps.shape)
    grad_rim = padded_2(conv_grad.astype(jnp.bfloat16), (("rows", 1),), 3).astype(conv_grad.dtype)
    grad_pad = jnp.pad(grad_rim, ((0, 0), (0, 0), (3, 3), (0, 0)))
    kernel_rows = []
    back_conv = jnp.zeros(feature_maps.shape, jnp.float32)
    for row_off in range(KS):
        for col_off in range(KS):
            window = padded[:, row_off : row_off + strip, col_off : col_off + across, :]
            kernel_rows.append(jnp.sum(window * conv_grad, axis=(0, 1, 2)))
            back_conv = (
                back_conv
                + grad_pad[
                    :, 6 - row_off : 6 - row_off + strip, 6 - col_off : 6 - col_off + across, :
                ]
                * dw_kernel[row_off, col_off]
            )
    kernel_part = jnp.stack(kernel_rows).reshape(KS, KS, width)
    grad_x = (d_out.astype(jnp.float32) + back_conv).astype(jnp.bfloat16)
    grad_kernel, grad_gain, grad_scale = small_sums(kernel_part, gain_part, scale_part, width)
    grad_sums, grad_x, grad_kernel, grad_gain, grad_scale = lax.optimization_barrier(
        (grad_sums, grad_x, grad_kernel, grad_gain, grad_scale)
    )
    grad_sums = lax.all_to_all(grad_sums, "rows", 1, 2, tiled=True).astype(jnp.float32)
    grad_up, grad_down = grad_sums[0], grad_sums[1].T
    return (result, grad_x, grad_up, grad_down, grad_kernel, grad_gain, grad_scale)


def solution(mesh):
    return jax.shard_map(
        body,
        mesh=mesh,
        in_specs=(
            P(("dp", "fsdp"), "rows", None, None),
            P(),
            P(),
            P(("dp", "rows"), "fsdp"),
            P("fsdp", ("dp", "rows")),
            P(),
            P(("dp", "fsdp"), "rows", None, None),
        ),
        out_specs=(
            P(("dp", "fsdp"), "rows", None, None),
            P(("dp", "fsdp"), "rows", None, None),
            P(("dp", "rows"), "fsdp"),
            P("fsdp", ("dp", "rows")),
            P(),
            P(),
            P(),
        ),
        check_vma=False,
    )
```

```python
import math

import jax
import jax.numpy as jnp
from jax import lax
from jax.sharding import PartitionSpec as P

KS = 7


norm_eps = 1e-06
inv_root_two = 1.0 / math.sqrt(2.0)
inv_root_two_pi = 1.0 / math.sqrt(2.0 * math.pi)
contract_rows = (((0,), (0,)), ((), ()))
contract_cols = (((1,), (1,)), ((), ()))


def padded_2(x, sides, width):
    for axis, dim in sides:
        devices, length = (lax.axis_size(axis), x.shape[dim])
        up = [(i, (i + 1) % devices) for i in range(devices - 1)]
        down = [(j, i) for i, j in up]
        last = lax.slice_in_dim(x, length - width, length, axis=dim)
        leading = lax.slice_in_dim(x, 0, width, axis=dim)
        before = lax.ppermute(last, axis, up)
        after = lax.ppermute(leading, axis, down)
        x = jnp.concatenate([before, x, after], axis=dim)
    return x


def gelu_exact(values):
    return 0.5 * values * (1.0 + jax.scipy.special.erf(values * inv_root_two))


def gelu_slope(values):
    cdf_part = 0.5 * (1.0 + jax.scipy.special.erf(values * inv_root_two))
    return cdf_part + values * jnp.exp(-0.5 * values * values) * inv_root_two_pi


def small_sums(kernel_part, gain_part, scale_part, width):
    every = ("dp", "fsdp", "rows")
    devices = lax.axis_size(every)
    packed = jnp.concatenate(
        [kernel_part.reshape(KS * KS, width), gain_part[None], scale_part[None]], axis=0
    )
    count = packed.shape[0]
    per = -(-count // devices)
    packed = jnp.pad(packed, ((0, per * devices - count), (0, 0)))
    mine = lax.all_to_all(packed.reshape(devices, per, width), every, 0, 0, tiled=True).sum(0)
    spread = jnp.broadcast_to(mine[None], (devices, per, width))
    total = lax.all_to_all(spread, every, 0, 0, tiled=True).reshape(devices * per, width)
    kernel_sum = total[: KS * KS].reshape(KS, KS, width)
    return kernel_sum, total[KS * KS], total[KS * KS + 1]


def body(feature_maps, dw_kernel, norm_gain, w_up, w_down, layer_scale, d_out):
    scenes, strip, across, width = feature_maps.shape
    cells = scenes * strip * across
    hid_axes = ("fsdp", "rows")
    dp_size, row_size = lax.axis_size("dp"), lax.axis_size("rows")
    block_c, hid_f = w_up.shape
    sub = hid_f // row_size
    pieces = w_up.reshape(block_c, row_size, sub).transpose(1, 0, 2)
    pieces = jnp.broadcast_to(pieces[None], (dp_size, row_size, block_c, sub))
    pieces = pieces.reshape(dp_size * row_size, block_c, sub)
    up_loc = lax.all_to_all(pieces, ("dp", "rows"), 0, 0, tiled=True)
    up_loc = up_loc.reshape(dp_size * row_size * block_c, sub)
    down_loc = lax.all_to_all(w_down, "rows", 0, 1, tiled=True)
    down_loc = lax.all_gather(down_loc, "dp", axis=1, tiled=True)
    cotan = d_out.reshape(cells, width).astype(jnp.float32)
    back = (cotan * layer_scale).astype(jnp.bfloat16)
    rimmed = padded_2(feature_maps, (("rows", 1),), 3)
    padded = jnp.pad(rimmed.astype(jnp.float32), ((0, 0), (0, 0), (3, 3), (0, 0)))
    filtered = jnp.zeros(feature_maps.shape, jnp.float32)
    for row_off in range(KS):
        for col_off in range(KS):
            filtered = (
                filtered
                + padded[:, row_off : row_off + strip, col_off : col_off + across, :]
                * dw_kernel[row_off, col_off]
            )
    flat = filtered.reshape(cells, width)
    average = jnp.mean(flat, axis=-1, keepdims=True)
    center = flat - average
    variance = jnp.mean(center * center, axis=-1, keepdims=True)
    rstd = lax.rsqrt(variance + norm_eps)
    normed = center * rstd
    scaled = (normed * norm_gain).astype(jnp.bfloat16)
    pair = lax.all_gather(jnp.stack([scaled, back]), hid_axes, axis=1, tiled=True)
    gathered, back_all = pair[0], pair[1]
    hidden = jnp.dot(gathered, up_loc, preferred_element_type=jnp.float32)
    active = gelu_exact(hidden).astype(jnp.bfloat16)
    mlp_terms = jnp.dot(active, down_loc, preferred_element_type=jnp.float32)
    down_part_t = lax.dot_general(
        back_all, active, contract_rows, preferred_element_type=jnp.float32
    )
    slope_in = lax.dot_general(
        back_all, down_loc, contract_cols, preferred_element_type=jnp.float32
    )
    hidden_grad = (slope_in * gelu_slope(hidden)).astype(jnp.bfloat16)
    up_part = lax.dot_general(
        gathered, hidden_grad, contract_rows, preferred_element_type=jnp.float32
    )
    norm_terms = lax.dot_general(
        hidden_grad, up_loc, contract_cols, preferred_element_type=jnp.float32
    )
    sums = lax.psum_scatter(
        jnp.stack([mlp_terms, norm_terms]).astype(jnp.bfloat16),
        hid_axes,
        scatter_dimension=1,
        tiled=True,
    ).astype(jnp.float32)
    branch, norm_grad = sums[0], sums[1]
    resid = feature_maps.reshape(cells, width).astype(jnp.float32)
    result = (resid + layer_scale * branch).astype(jnp.bfloat16).reshape(feature_maps.shape)
    scale_part = jnp.sum(cotan * branch, axis=0)
    down_blocks = down_part_t.astype(jnp.bfloat16).reshape(dp_size, -1, sub)
    down_sum = lax.all_to_all(down_blocks, "dp", 0, 0, tiled=True).astype(jnp.float32).sum(0)
    up_sum = lax.psum_scatter(
        up_part.astype(jnp.bfloat16), "dp", scatter_dimension=0, tiled=True
    )
    grad_sums = jnp.stack([up_sum, down_sum.astype(jnp.bfloat16)])
    gain_part = jnp.sum(norm_grad * normed, axis=0)
    scaled_grad = norm_grad * norm_gain
    conv_grad = rstd * (
        scaled_grad
        - jnp.mean(scaled_grad, axis=-1, keepdims=True)
        - normed * jnp.mean(scaled_grad * normed, axis=-1, keepdims=True)
    )
    conv_grad = conv_grad.reshape(feature_maps.shape)
    grad_rim = padded_2(conv_grad.astype(jnp.bfloat16), (("rows", 1),), 3).astype(conv_grad.dtype)
    grad_pad = jnp.pad(grad_rim, ((0, 0), (0, 0), (3, 3), (0, 0)))
    kernel_rows = []
    back_conv = jnp.zeros(feature_maps.shape, jnp.float32)
    for row_off in range(KS):
        for col_off in range(KS):
            window = padded[:, row_off : row_off + strip, col_off : col_off + across, :]
            kernel_rows.append(jnp.sum(window * conv_grad, axis=(0, 1, 2)))
            back_conv = (
                back_conv
                + grad_pad[
                    :, 6 - row_off : 6 - row_off + strip, 6 - col_off : 6 - col_off + across, :
                ]
                * dw_kernel[row_off, col_off]
            )
    kernel_part = jnp.stack(kernel_rows).reshape(KS, KS, width)
    grad_x = (d_out.astype(jnp.float32) + back_conv).astype(jnp.bfloat16)
    grad_kernel, grad_gain, grad_scale = small_sums(kernel_part, gain_part, scale_part, width)
    grad_sums, grad_x, grad_kernel, grad_gain, grad_scale = lax.optimization_barrier(
        (grad_sums, grad_x, grad_kernel, grad_gain, grad_scale)
    )
    grad_sums = lax.all_to_all(grad_sums, "rows", 1, 2, tiled=True).astype(jnp.float32)
    grad_up, grad_down = grad_sums[0], grad_sums[1].T
    return (result, grad_x, grad_up, grad_down, grad_kernel, grad_gain, grad_scale)


def solution(mesh):
    return jax.shard_map(
        body,
        mesh=mesh,
        in_specs=(
            P(("dp", "fsdp"), "rows", None, None),
            P(),
            P(),
            P(("dp", "rows"), "fsdp"),
            P("fsdp", ("dp", "rows")),
            P(),
            P(("dp", "fsdp"), "rows", None, None),
        ),
        out_specs=(
            P(("dp", "fsdp"), "rows", None, None),
            P(("dp", "fsdp"), "rows", None, None),
            P(("dp", "rows"), "fsdp"),
            P("fsdp", ("dp", "rows")),
            P(),
            P(),
            P(),
        ),
        check_vma=False,
    )
```

```python
import math

import jax
import jax.numpy as jnp
from jax import lax
from jax.sharding import PartitionSpec as P

KS = 7


norm_eps = 1e-06
inv_root_two = 1.0 / math.sqrt(2.0)
inv_root_two_pi = 1.0 / math.sqrt(2.0 * math.pi)
contract_rows = (((0,), (0,)), ((), ()))
contract_cols = (((1,), (1,)), ((), ()))


def padded_2(x, sides, width):
    for axis, dim in sides:
        devices, length = (lax.axis_size(axis), x.shape[dim])
        up = [(i, (i + 1) % devices) for i in range(devices - 1)]
        down = [(j, i) for i, j in up]
        last = lax.slice_in_dim(x, length - width, length, axis=dim)
        leading = lax.slice_in_dim(x, 0, width, axis=dim)
        before = lax.ppermute(last, axis, up)
        after = lax.ppermute(leading, axis, down)
        x = jnp.concatenate([before, x, after], axis=dim)
    return x


def gelu_exact(values):
    return 0.5 * values * (1.0 + jax.scipy.special.erf(values * inv_root_two))


def gelu_slope(values):
    cdf_part = 0.5 * (1.0 + jax.scipy.special.erf(values * inv_root_two))
    return cdf_part + values * jnp.exp(-0.5 * values * values) * inv_root_two_pi


def small_sums(kernel_part, gain_part, scale_part, width):
    every = ("dp", "fsdp", "rows")
    devices = lax.axis_size(every)
    packed = jnp.concatenate(
        [kernel_part.reshape(KS * KS, width), gain_part[None], scale_part[None]], axis=0
    )
    count = packed.shape[0]
    per = -(-count // devices)
    packed = jnp.pad(packed, ((0, per * devices - count), (0, 0)))
    mine = lax.all_to_all(packed.reshape(devices, per, width), every, 0, 0, tiled=True).sum(0)
    spread = jnp.broadcast_to(mine[None], (devices, per, width))
    total = lax.all_to_all(spread, every, 0, 0, tiled=True).reshape(devices * per, width)
    kernel_sum = total[: KS * KS].reshape(KS, KS, width)
    return kernel_sum, total[KS * KS], total[KS * KS + 1]


def body(feature_maps, dw_kernel, norm_gain, w_up, w_down, layer_scale, d_out):
    scenes, strip, across, width = feature_maps.shape
    cells = scenes * strip * across
    hid_axes = ("fsdp", "rows")
    dp_size, row_size = lax.axis_size("dp"), lax.axis_size("rows")
    block_c, hid_f = w_up.shape
    sub = hid_f // row_size
    pieces = w_up.reshape(block_c, row_size, sub).transpose(1, 0, 2)
    pieces = jnp.broadcast_to(pieces[None], (dp_size, row_size, block_c, sub))
    pieces = pieces.reshape(dp_size * row_size, block_c, sub)
    up_loc = lax.all_to_all(pieces, ("dp", "rows"), 0, 0, tiled=True)
    up_loc = up_loc.reshape(dp_size * row_size * block_c, sub)
    down_loc = lax.all_to_all(w_down, "rows", 0, 1, tiled=True)
    down_loc = lax.all_gather(down_loc, "dp", axis=1, tiled=True)
    cotan = d_out.reshape(cells, width).astype(jnp.float32)
    back = (cotan * layer_scale).astype(jnp.bfloat16)
    rimmed = padded_2(feature_maps, (("rows", 1),), 3)
    padded = jnp.pad(rimmed.astype(jnp.float32), ((0, 0), (0, 0), (3, 3), (0, 0)))
    filtered = jnp.zeros(feature_maps.shape, jnp.float32)
    for row_off in range(KS):
        for col_off in range(KS):
            filtered = (
                filtered
                + padded[:, row_off : row_off + strip, col_off : col_off + across, :]
                * dw_kernel[row_off, col_off]
            )
    flat = filtered.reshape(cells, width)
    average = jnp.mean(flat, axis=-1, keepdims=True)
    center = flat - average
    variance = jnp.mean(center * center, axis=-1, keepdims=True)
    rstd = lax.rsqrt(variance + norm_eps)
    normed = center * rstd
    scaled = (normed * norm_gain).astype(jnp.bfloat16)
    pair = lax.all_gather(jnp.stack([scaled, back]), hid_axes, axis=1, tiled=True)
    gathered, back_all = pair[0], pair[1]
    hidden = jnp.dot(gathered, up_loc, preferred_element_type=jnp.float32)
    active = gelu_exact(hidden).astype(jnp.bfloat16)
    mlp_terms = jnp.dot(active, down_loc, preferred_element_type=jnp.float32)
    down_part_t = lax.dot_general(
        back_all, active, contract_rows, preferred_element_type=jnp.float32
    )
    slope_in = lax.dot_general(
        back_all, down_loc, contract_cols, preferred_element_type=jnp.float32
    )
    hidden_grad = (slope_in * gelu_slope(hidden)).astype(jnp.bfloat16)
    up_part = lax.dot_general(
        gathered, hidden_grad, contract_rows, preferred_element_type=jnp.float32
    )
    norm_terms = lax.dot_general(
        hidden_grad, up_loc, contract_cols, preferred_element_type=jnp.float32
    )
    sums = lax.psum_scatter(
        jnp.stack([mlp_terms, norm_terms]).astype(jnp.bfloat16),
        hid_axes,
        scatter_dimension=1,
        tiled=True,
    ).astype(jnp.float32)
    branch, norm_grad = sums[0], sums[1]
    resid = feature_maps.reshape(cells, width).astype(jnp.float32)
    result = (resid + layer_scale * branch).astype(jnp.bfloat16).reshape(feature_maps.shape)
    scale_part = jnp.sum(cotan * branch, axis=0)
    def rows_first(part):
        part = part.astype(jnp.bfloat16).reshape(dp_size, row_size, block_c, sub)
        part = lax.all_to_all(part, "rows", 1, 3, tiled=True)
        return part.reshape(dp_size, block_c, row_size * sub)

    down_sum = lax.all_to_all(rows_first(down_part_t), "dp", 0, 0, tiled=True)
    down_sum = down_sum.astype(jnp.float32).sum(0)
    up_sum = lax.psum_scatter(rows_first(up_part), "dp", scatter_dimension=0, tiled=True)
    grad_sums = (up_sum.reshape(block_c, row_size * sub), down_sum)
    gain_part = jnp.sum(norm_grad * normed, axis=0)
    scaled_grad = norm_grad * norm_gain
    conv_grad = rstd * (
        scaled_grad
        - jnp.mean(scaled_grad, axis=-1, keepdims=True)
        - normed * jnp.mean(scaled_grad * normed, axis=-1, keepdims=True)
    )
    conv_grad = conv_grad.reshape(feature_maps.shape)
    grad_rim = padded_2(conv_grad.astype(jnp.bfloat16), (("rows", 1),), 3).astype(conv_grad.dtype)
    grad_pad = jnp.pad(grad_rim, ((0, 0), (0, 0), (3, 3), (0, 0)))
    kernel_rows = []
    back_conv = jnp.zeros(feature_maps.shape, jnp.float32)
    for row_off in range(KS):
        for col_off in range(KS):
            window = padded[:, row_off : row_off + strip, col_off : col_off + across, :]
            kernel_rows.append(jnp.sum(window * conv_grad, axis=(0, 1, 2)))
            back_conv = (
                back_conv
                + grad_pad[
                    :, 6 - row_off : 6 - row_off + strip, 6 - col_off : 6 - col_off + across, :
                ]
                * dw_kernel[row_off, col_off]
            )
    kernel_part = jnp.stack(kernel_rows).reshape(KS, KS, width)
    grad_x = (d_out.astype(jnp.float32) + back_conv).astype(jnp.bfloat16)
    grad_kernel, grad_gain, grad_scale = small_sums(kernel_part, gain_part, scale_part, width)
    grad_sums, grad_x, grad_kernel, grad_gain, grad_scale = lax.optimization_barrier(
        (grad_sums, grad_x, grad_kernel, grad_gain, grad_scale)
    )
    grad_up, grad_down = grad_sums[0].astype(jnp.float32), grad_sums[1].T
    return (result, grad_x, grad_up, grad_down, grad_kernel, grad_gain, grad_scale)


def solution(mesh):
    return jax.shard_map(
        body,
        mesh=mesh,
        in_specs=(
            P(("dp", "fsdp"), "rows", None, None),
            P(),
            P(),
            P(("dp", "rows"), "fsdp"),
            P("fsdp", ("dp", "rows")),
            P(),
            P(("dp", "fsdp"), "rows", None, None),
        ),
        out_specs=(
            P(("dp", "fsdp"), "rows", None, None),
            P(("dp", "fsdp"), "rows", None, None),
            P(("dp", "rows"), "fsdp"),
            P("fsdp", ("dp", "rows")),
            P(),
            P(),
            P(),
        ),
        check_vma=False,
    )
```

```python
import math

import jax
import jax.numpy as jnp
from jax import lax
from jax.sharding import PartitionSpec as P

KS = 7


norm_eps = 1e-06
inv_root_two = 1.0 / math.sqrt(2.0)
inv_root_two_pi = 1.0 / math.sqrt(2.0 * math.pi)
contract_rows = (((0,), (0,)), ((), ()))
contract_cols = (((1,), (1,)), ((), ()))


def padded_2(x, sides, width):
    for axis, dim in sides:
        devices, length = (lax.axis_size(axis), x.shape[dim])
        up = [(i, (i + 1) % devices) for i in range(devices - 1)]
        down = [(j, i) for i, j in up]
        last = lax.slice_in_dim(x, length - width, length, axis=dim)
        leading = lax.slice_in_dim(x, 0, width, axis=dim)
        before = lax.ppermute(last, axis, up)
        after = lax.ppermute(leading, axis, down)
        x = jnp.concatenate([before, x, after], axis=dim)
    return x


def gelu_exact(values):
    return 0.5 * values * (1.0 + jax.scipy.special.erf(values * inv_root_two))


def gelu_slope(values):
    cdf_part = 0.5 * (1.0 + jax.scipy.special.erf(values * inv_root_two))
    return cdf_part + values * jnp.exp(-0.5 * values * values) * inv_root_two_pi


def small_sums(kernel_part, gain_part, scale_part, width):
    every = ("dp", "fsdp", "rows")
    devices = lax.axis_size(every)
    packed = jnp.concatenate(
        [kernel_part.reshape(KS * KS, width), gain_part[None], scale_part[None]], axis=0
    )
    count = packed.shape[0]
    per = -(-count // devices)
    packed = jnp.pad(packed, ((0, per * devices - count), (0, 0)))
    mine = lax.all_to_all(packed.reshape(devices, per, width), every, 0, 0, tiled=True).sum(0)
    spread = jnp.broadcast_to(mine[None], (devices, per, width))
    total = lax.all_to_all(spread, every, 0, 0, tiled=True).reshape(devices * per, width)
    kernel_sum = total[: KS * KS].reshape(KS, KS, width)
    return kernel_sum, total[KS * KS], total[KS * KS + 1]


def body(feature_maps, dw_kernel, norm_gain, w_up, w_down, layer_scale, d_out):
    scenes, strip, across, width = feature_maps.shape
    cells = scenes * strip * across
    hid_axes = ("fsdp", "rows")
    dp_size, row_size = lax.axis_size("dp"), lax.axis_size("rows")
    block_c, hid_f = w_up.shape
    sub = hid_f // row_size
    pieces = w_up.reshape(block_c, row_size, sub).transpose(1, 0, 2)
    pieces = jnp.broadcast_to(pieces[None], (dp_size, row_size, block_c, sub))
    pieces = pieces.reshape(dp_size * row_size, block_c, sub)
    up_loc = lax.all_to_all(pieces, ("dp", "rows"), 0, 0, tiled=True)
    up_loc = up_loc.reshape(dp_size * row_size * block_c, sub)
    down_loc = lax.all_to_all(w_down, "rows", 0, 1, tiled=True)
    down_loc = lax.all_gather(down_loc, "dp", axis=1, tiled=True)
    cotan = d_out.reshape(cells, width).astype(jnp.float32)
    back = (cotan * layer_scale).astype(jnp.bfloat16)
    rimmed = padded_2(feature_maps, (("rows", 1),), 3)
    padded = jnp.pad(rimmed.astype(jnp.float32), ((0, 0), (0, 0), (3, 3), (0, 0)))
    filtered = jnp.zeros(feature_maps.shape, jnp.float32)
    for row_off in range(KS):
        for col_off in range(KS):
            filtered = (
                filtered
                + padded[:, row_off : row_off + strip, col_off : col_off + across, :]
                * dw_kernel[row_off, col_off]
            )
    flat = filtered.reshape(cells, width)
    average = jnp.mean(flat, axis=-1, keepdims=True)
    center = flat - average
    variance = jnp.mean(center * center, axis=-1, keepdims=True)
    rstd = lax.rsqrt(variance + norm_eps)
    normed = center * rstd
    scaled = (normed * norm_gain).astype(jnp.bfloat16)
    pair = lax.all_gather(jnp.stack([scaled, back]), hid_axes, axis=1, tiled=True)
    gathered, back_all = pair[0], pair[1]
    hidden = jnp.dot(gathered, up_loc, preferred_element_type=jnp.float32)
    active = gelu_exact(hidden).astype(jnp.bfloat16)
    mlp_terms = jnp.dot(active, down_loc, preferred_element_type=jnp.float32)
    down_part_t = lax.dot_general(
        back_all, active, contract_rows, preferred_element_type=jnp.float32
    )
    slope_in = lax.dot_general(
        back_all, down_loc, contract_cols, preferred_element_type=jnp.float32
    )
    hidden_grad = (slope_in * gelu_slope(hidden)).astype(jnp.bfloat16)
    up_part = lax.dot_general(
        gathered, hidden_grad, contract_rows, preferred_element_type=jnp.float32
    )
    norm_terms = lax.dot_general(
        hidden_grad, up_loc, contract_cols, preferred_element_type=jnp.float32
    )
    sums = lax.psum_scatter(
        jnp.stack([mlp_terms, norm_terms]).astype(jnp.bfloat16),
        hid_axes,
        scatter_dimension=1,
        tiled=True,
    ).astype(jnp.float32)
    branch, norm_grad = sums[0], sums[1]
    resid = feature_maps.reshape(cells, width).astype(jnp.float32)
    result = (resid + layer_scale * branch).astype(jnp.bfloat16).reshape(feature_maps.shape)
    scale_part = jnp.sum(cotan * branch, axis=0)
    blocks = jnp.stack([up_part, down_part_t]).astype(jnp.bfloat16).reshape(2, dp_size, -1, sub)
    grad_sums = lax.all_to_all(blocks, "dp", 1, 1, tiled=True).astype(jnp.float32).sum(1)
    grad_sums = grad_sums.astype(jnp.bfloat16)
    gain_part = jnp.sum(norm_grad * normed, axis=0)
    scaled_grad = norm_grad * norm_gain
    conv_grad = rstd * (
        scaled_grad
        - jnp.mean(scaled_grad, axis=-1, keepdims=True)
        - normed * jnp.mean(scaled_grad * normed, axis=-1, keepdims=True)
    )
    conv_grad = conv_grad.reshape(feature_maps.shape)
    grad_rim = padded_2(conv_grad.astype(jnp.bfloat16), (("rows", 1),), 3).astype(conv_grad.dtype)
    grad_pad = jnp.pad(grad_rim, ((0, 0), (0, 0), (3, 3), (0, 0)))
    kernel_rows = []
    back_conv = jnp.zeros(feature_maps.shape, jnp.float32)
    for row_off in range(KS):
        for col_off in range(KS):
            window = padded[:, row_off : row_off + strip, col_off : col_off + across, :]
            kernel_rows.append(jnp.sum(window * conv_grad, axis=(0, 1, 2)))
            back_conv = (
                back_conv
                + grad_pad[
                    :, 6 - row_off : 6 - row_off + strip, 6 - col_off : 6 - col_off + across, :
                ]
                * dw_kernel[row_off, col_off]
            )
    kernel_part = jnp.stack(kernel_rows).reshape(KS, KS, width)
    grad_x = (d_out.astype(jnp.float32) + back_conv).astype(jnp.bfloat16)
    grad_kernel, grad_gain, grad_scale = small_sums(kernel_part, gain_part, scale_part, width)
    grad_sums, grad_x, grad_kernel, grad_gain, grad_scale = lax.optimization_barrier(
        (grad_sums, grad_x, grad_kernel, grad_gain, grad_scale)
    )
    grad_sums = lax.all_to_all(grad_sums, "rows", 1, 2, tiled=True).astype(jnp.float32)
    grad_up, grad_down = grad_sums[0], grad_sums[1].T
    return (result, grad_x, grad_up, grad_down, grad_kernel, grad_gain, grad_scale)


def solution(mesh):
    return jax.shard_map(
        body,
        mesh=mesh,
        in_specs=(
            P(("dp", "fsdp"), "rows", None, None),
            P(),
            P(),
            P(("dp", "rows"), "fsdp"),
            P("fsdp", ("dp", "rows")),
            P(),
            P(("dp", "fsdp"), "rows", None, None),
        ),
        out_specs=(
            P(("dp", "fsdp"), "rows", None, None),
            P(("dp", "fsdp"), "rows", None, None),
            P(("dp", "rows"), "fsdp"),
            P("fsdp", ("dp", "rows")),
            P(),
            P(),
            P(),
        ),
        check_vma=False,
    )
```

```python
import math

import jax
import jax.numpy as jnp
from jax import lax
from jax.sharding import PartitionSpec as P

KS = 7


norm_eps = 1e-06
inv_root_two = 1.0 / math.sqrt(2.0)
inv_root_two_pi = 1.0 / math.sqrt(2.0 * math.pi)
contract_rows = (((0,), (0,)), ((), ()))
contract_cols = (((1,), (1,)), ((), ()))


def padded_2(x, sides, width):
    for axis, dim in sides:
        devices, length = (lax.axis_size(axis), x.shape[dim])
        up = [(i, (i + 1) % devices) for i in range(devices - 1)]
        down = [(j, i) for i, j in up]
        last = lax.slice_in_dim(x, length - width, length, axis=dim)
        leading = lax.slice_in_dim(x, 0, width, axis=dim)
        before = lax.ppermute(last, axis, up)
        after = lax.ppermute(leading, axis, down)
        x = jnp.concatenate([before, x, after], axis=dim)
    return x


def gelu_exact(values):
    return 0.5 * values * (1.0 + jax.scipy.special.erf(values * inv_root_two))


def gelu_slope(values):
    cdf_part = 0.5 * (1.0 + jax.scipy.special.erf(values * inv_root_two))
    return cdf_part + values * jnp.exp(-0.5 * values * values) * inv_root_two_pi


def small_sums(kernel_part, gain_part, scale_part, width):
    every = ("dp", "fsdp", "rows")
    devices = lax.axis_size(every)
    packed = jnp.concatenate(
        [kernel_part.reshape(KS * KS, width), gain_part[None], scale_part[None]], axis=0
    )
    count = packed.shape[0]
    per = -(-count // devices)
    packed = jnp.pad(packed, ((0, per * devices - count), (0, 0)))
    mine = lax.all_to_all(packed.reshape(devices, per, width), every, 0, 0, tiled=True).sum(0)
    spread = jnp.broadcast_to(mine[None], (devices, per, width))
    total = lax.all_to_all(spread, every, 0, 0, tiled=True).reshape(devices * per, width)
    kernel_sum = total[: KS * KS].reshape(KS, KS, width)
    return kernel_sum, total[KS * KS], total[KS * KS + 1]


def body(feature_maps, dw_kernel, norm_gain, w_up, w_down, layer_scale, d_out):
    scenes, strip, across, width = feature_maps.shape
    cells = scenes * strip * across
    hid_axes = ("fsdp", "rows")
    dp_size, row_size = lax.axis_size("dp"), lax.axis_size("rows")
    block_c, hid_f = w_up.shape
    sub = hid_f // row_size
    pieces = w_up.reshape(block_c, row_size, sub).transpose(1, 0, 2)
    pieces = jnp.broadcast_to(pieces[None], (dp_size, row_size, block_c, sub))
    pieces = pieces.reshape(dp_size * row_size, block_c, sub)
    up_loc = lax.all_to_all(pieces, ("dp", "rows"), 0, 0, tiled=True)
    up_loc = up_loc.reshape(dp_size * row_size * block_c, sub)
    down_loc = lax.all_to_all(w_down, "rows", 0, 1, tiled=True)
    down_loc = lax.all_gather(down_loc, "dp", axis=1, tiled=True)
    cotan = d_out.reshape(cells, width).astype(jnp.float32)
    back = (cotan * layer_scale).astype(jnp.bfloat16)
    rimmed = padded_2(feature_maps, (("rows", 1),), 3)
    padded = jnp.pad(rimmed.astype(jnp.float32), ((0, 0), (0, 0), (3, 3), (0, 0)))
    filtered = jnp.zeros(feature_maps.shape, jnp.float32)
    for row_off in range(KS):
        for col_off in range(KS):
            filtered = (
                filtered
                + padded[:, row_off : row_off + strip, col_off : col_off + across, :]
                * dw_kernel[row_off, col_off]
            )
    flat = filtered.reshape(cells, width)
    average = jnp.mean(flat, axis=-1, keepdims=True)
    center = flat - average
    variance = jnp.mean(center * center, axis=-1, keepdims=True)
    rstd = lax.rsqrt(variance + norm_eps)
    normed = center * rstd
    scaled = (normed * norm_gain).astype(jnp.bfloat16)
    pair = lax.all_gather(jnp.stack([scaled, back]), hid_axes, axis=1, tiled=True)
    gathered, back_all = pair[0], pair[1]
    hidden = jnp.dot(gathered, up_loc, preferred_element_type=jnp.float32)
    active = gelu_exact(hidden).astype(jnp.bfloat16)
    mlp_terms = jnp.dot(active, down_loc, preferred_element_type=jnp.float32)
    down_part_t = lax.dot_general(
        back_all, active, contract_rows, preferred_element_type=jnp.float32
    )
    slope_in = lax.dot_general(
        back_all, down_loc, contract_cols, preferred_element_type=jnp.float32
    )
    hidden_grad = (slope_in * gelu_slope(hidden)).astype(jnp.bfloat16)
    up_part = lax.dot_general(
        gathered, hidden_grad, contract_rows, preferred_element_type=jnp.float32
    )
    norm_terms = lax.dot_general(
        hidden_grad, up_loc, contract_cols, preferred_element_type=jnp.float32
    )
    sums = lax.psum_scatter(
        jnp.stack([mlp_terms, norm_terms]).astype(jnp.bfloat16),
        hid_axes,
        scatter_dimension=1,
        tiled=True,
    ).astype(jnp.float32)
    branch, norm_grad = sums[0], sums[1]
    resid = feature_maps.reshape(cells, width).astype(jnp.float32)
    result = (resid + layer_scale * branch).astype(jnp.bfloat16).reshape(feature_maps.shape)
    scale_part = jnp.sum(cotan * branch, axis=0)
    down_blocks = down_part_t.astype(jnp.bfloat16).reshape(dp_size, -1, sub)
    down_sum = lax.all_to_all(down_blocks, "dp", 0, 0, tiled=True).astype(jnp.float32).sum(0)
    up_sum = lax.psum_scatter(
        up_part.astype(jnp.bfloat16), "dp", scatter_dimension=0, tiled=True
    )
    grad_sums = jnp.stack([up_sum, down_sum.astype(jnp.bfloat16)])
    gain_part = jnp.sum(norm_grad * normed, axis=0)
    scaled_grad = norm_grad * norm_gain
    conv_grad = rstd * (
        scaled_grad
        - jnp.mean(scaled_grad, axis=-1, keepdims=True)
        - normed * jnp.mean(scaled_grad * normed, axis=-1, keepdims=True)
    )
    conv_grad = conv_grad.reshape(feature_maps.shape)
    grad_rim = padded_2(conv_grad.astype(jnp.bfloat16), (("rows", 1),), 3).astype(conv_grad.dtype)
    grad_pad = jnp.pad(grad_rim, ((0, 0), (0, 0), (3, 3), (0, 0)))
    kernel_rows = []
    back_conv = jnp.zeros(feature_maps.shape, jnp.float32)
    for row_off in range(KS):
        for col_off in range(KS):
            window = padded[:, row_off : row_off + strip, col_off : col_off + across, :]
            kernel_rows.append(jnp.sum(window * conv_grad, axis=(0, 1, 2)))
            back_conv = (
                back_conv
                + grad_pad[
                    :, 6 - row_off : 6 - row_off + strip, 6 - col_off : 6 - col_off + across, :
                ]
                * dw_kernel[row_off, col_off]
            )
    kernel_part = jnp.stack(kernel_rows).reshape(KS, KS, width)
    grad_x = (d_out.astype(jnp.float32) + back_conv).astype(jnp.bfloat16)
    grad_kernel, grad_gain, grad_scale = small_sums(kernel_part, gain_part, scale_part, width)
    grad_sums = lax.all_to_all(grad_sums, "rows", 1, 2, tiled=True).astype(jnp.float32)
    grad_up, grad_down = grad_sums[0], grad_sums[1].T
    return (result, grad_x, grad_up, grad_down, grad_kernel, grad_gain, grad_scale)


def solution(mesh):
    return jax.shard_map(
        body,
        mesh=mesh,
        in_specs=(
            P(("dp", "fsdp"), "rows", None, None),
            P(),
            P(),
            P(("dp", "rows"), "fsdp"),
            P("fsdp", ("dp", "rows")),
            P(),
            P(("dp", "fsdp"), "rows", None, None),
        ),
        out_specs=(
            P(("dp", "fsdp"), "rows", None, None),
            P(("dp", "fsdp"), "rows", None, None),
            P(("dp", "rows"), "fsdp"),
            P("fsdp", ("dp", "rows")),
            P(),
            P(),
            P(),
        ),
        check_vma=False,
    )
```
